256 devices in a mesh: grp: 8 (over y, z_hi), tile: 32 (over z_lo, x, core).
Axes of the slice: x: 4, y: 4, z: 8 (z_hi: 2, z_lo: 4; z = z_hi * 4 + z_lo), core: 2. Of those that a mesh axis runs over, the one named last changes fastest.
Arguments:
- sensitivity: bfloat16 [16, 4096, 3, 1024], P('grp', 'tile'), may hold values from -6 to 6
- inst_weight: float32 [16], P('grp'), may hold values from 0.3 to 3
- filter_taps: bfloat16 [129], replicated, may hold values from 0.019897461 to 0.13964844
- basis_rows: bfloat16 [128, 16], replicated, may hold values from -0.5 to 0.5
- basis_cols: bfloat16 [128, 16], replicated, may hold values from -0.5 to 0.5
- box_table: int32 [256, 1], replicated, may hold values from 0 to 255
- owner_perm: int32 [256], replicated, may hold values from 0 to 255, each once
Outputs:
- design_grad: float32 [256, 3, 256], P(('grp', 'tile'))
The draws below stay inside these ranges and needn't reach their ends.
Inputs may be any that keep to these rules, and one draw needn't show every extreme that they name: `box_table`: every one of the 256 boxes is named by at least one tile. `owner_perm`: each box appears exactly once.
All inputs are finite; a program needn't handle non-finite values.
Results may differ from the reference program's by a relative error of at most 0.017.
Values may be sent and summed in bfloat16 or wider, within the bound.
No kernel may reach another device: no remote copies, remote signals or barrier semaphores. Data moves between devices by JAX's collectives and lax.ppermute only.
A program may use at most 64 MiB of HBM per device.

```python
import math
import jax
import jax.numpy as jnp
from jax import lax

G2 = 1024
INST_GRP = 2
TAPS = 129
TR = 128
TC = 128
KR = 16
KC = 16
G1 = 4096
INSTANCES = 16
NB = 256
NTILES = 256


def block_scale(key, dims, pieces, low, top_value):
    loudness = 1.0
    for dim, shards_of in pieces:
        steps = jax.random.uniform(jax.random.fold_in(jax.random.fold_in(key, 6), dim), (shards_of,), jnp.float32, low / len(pieces), top_value / len(pieces))
        loudness = loudness * jnp.repeat(jnp.exp(steps), dims[dim] // shards_of).reshape((-1,) + (1,) * (len(dims) - 1 - dim))
    return loudness


def distinct(key, rows, count, top, lift):
    sequence = jax.random.permutation(jax.random.fold_in(key, 1), count)
    boost = sequence
    for power in range(3):
        boost = boost * boost // count
    boost = boost * lift // count
    lots = jax.random.randint(jax.random.fold_in(key, 2), (rows, count), 0, 4096) + boost
    sure = jax.random.permutation(jax.random.fold_in(key, 3), rows)[jnp.arange(count) % rows]
    lots = jnp.where(jnp.arange(rows)[:, None] == sure[None, :], 1 << 14, lots)
    merit = lots * count + jnp.arange(count)
    return lax.top_k(merit.astype(jnp.int32), top)[1].astype(jnp.int32)


def scatter_about(own_key, shape, deviation, limit, shards=(), kind=jnp.bfloat16):
    level = block_scale(own_key, shape, shards, -0.22, 0.18) if shards else 1.0
    entries = jax.random.normal(own_key, shape, jnp.float32) * deviation * level
    return jnp.minimum(jnp.maximum(entries, -limit), limit).astype(kind)


def setup_inputs(seed: int = 0) -> dict:
    seeds = jax.random.split(jax.random.key(seed), 8)
    return {
        "sensitivity": scatter_about(seeds[0], (INSTANCES, G1, 3, G2), 1.0, 6.0, ((0, 8), (1, 32))),
        "inst_weight": jnp.clip(jnp.exp(math.log(3.0) - 2.3025851 * jax.random.uniform(seeds[1], (INSTANCES,), jnp.float32) ** block_scale(seeds[1], (INSTANCES,), ((0, 8),), -0.2, 0.2)), 0.3, 3.0),
        "filter_taps": jnp.clip(jax.random.uniform(seeds[2], (TAPS,), jnp.float32, 0.019897461, 0.13964844), 0.019897461, 0.13964844).astype(jnp.bfloat16),
        "basis_rows": scatter_about(seeds[3], (TR, KR), TR ** -0.5, 0.5),
        "basis_cols": scatter_about(seeds[4], (TC, KC), TC ** -0.5, 0.5),
        "box_table": distinct(seeds[5], NTILES, NB, 1, 0),
        "owner_perm": jax.random.permutation(seeds[6], NB).astype(jnp.int32),
    }


def smooth_axis(field, filter_taps, axis):
    reach = filter_taps.shape[0] - 1
    half = reach // 2
    length = field.shape[axis]
    widths = [(0, 0)] * field.ndim
    widths[axis] = (half, half)
    padded = jnp.pad(field.astype(jnp.float32), widths)
    weights = filter_taps.astype(jnp.float32)
    total = jnp.zeros(field.shape, jnp.float32)
    for offset in range(reach + 1):
        total = total + weights[offset] * lax.slice_in_dim(padded, offset, offset + length, axis=axis)
    return total.astype(jnp.bfloat16)


def reference(sensitivity, inst_weight, filter_taps, basis_rows, basis_cols, box_table, owner_perm):
    rows_all = sensitivity.shape[1]
    cols_all = sensitivity.shape[3]
    groups = sensitivity.shape[0] // INST_GRP
    boxes = owner_perm.shape[0]
    grouped = sensitivity.reshape(groups, INST_GRP, rows_all, 3, cols_all)
    weights = inst_weight.reshape(groups, INST_GRP)

    def one_group(pair):
        block, weight = pair
        summed = jnp.sum(block.astype(jnp.float32) * weight[:, None, None, None], axis=0).astype(jnp.bfloat16)
        first = smooth_axis(summed, filter_taps, 2)
        second = smooth_axis(first, filter_taps, 0)
        tiles = second.reshape(rows_all // TR, TR, 3, cols_all // TC, TC).astype(jnp.float32)
        rowwise = jnp.einsum("xakyc,ap->xykpc", tiles, basis_rows.astype(jnp.float32), precision=lax.Precision.HIGHEST)
        tile_part = jnp.einsum("xykpc,cq->xykpq", rowwise, basis_cols.astype(jnp.float32), precision=lax.Precision.HIGHEST)
        flat = tile_part.reshape(-1, 3 * KR * KC)
        return jax.ops.segment_sum(flat, box_table[:, 0], num_segments=boxes)

    box_grad = jnp.sum(lax.map(one_group, (grouped, weights)), axis=0)
    return box_grad[owner_perm].reshape(boxes, 3, KR * KC)
```

```python
import jax
import jax.numpy as jnp
from jax import lax
from jax.sharding import PartitionSpec as P


def smoothed_basis(filter_taps, basis):
    reach = filter_taps.shape[0] - 1
    length = basis.shape[0]
    span = length + 2 * (reach // 2)
    offs = jnp.arange(span, dtype=jnp.int32)[:, None] - jnp.arange(length, dtype=jnp.int32)[None, :]
    taps = filter_taps.astype(jnp.float32)
    band = jnp.where((offs >= 0) & (offs <= reach), taps[jnp.clip(offs, 0, reach)], 0.0)
    return jnp.dot(band, basis.astype(jnp.float32), precision=lax.Precision.HIGHEST)


def window_blocks(extended, length):
    half = (extended.shape[0] - length) // 2
    padded = jnp.pad(extended, ((length - half, length - half), (0, 0)))
    return padded.reshape(3, length, -1)


def local(sensitivity, inst_weight, filter_taps, basis_rows, basis_cols, box_table, owner_perm):
    tile_rows, ctrl_rows = basis_rows.shape
    tile_cols, ctrl_cols = basis_cols.shape
    local_rows = sensitivity.shape[1]
    cols_all = sensitivity.shape[3]
    col_tiles = cols_all // tile_cols
    comps = sensitivity.shape[2]
    slots = owner_perm.shape[0]

    summed = jnp.sum(
        sensitivity.astype(jnp.float32) * inst_weight[:, None, None, None], axis=0
    ).astype(jnp.bfloat16)

    col_blocks = window_blocks(smoothed_basis(filter_taps, basis_cols), tile_cols)
    col_shift = (
        jnp.arange(col_tiles, dtype=jnp.int32)[:, None]
        - jnp.arange(col_tiles, dtype=jnp.int32)[None, :]
        + 1
    )
    col_valid = (col_shift >= 0) & (col_shift <= 2)
    col_matrix = jnp.where(
        col_valid[:, None, :, None],
        col_blocks[jnp.clip(col_shift, 0, 2)].transpose(0, 2, 1, 3),
        0.0,
    ).reshape(cols_all, col_tiles * ctrl_cols)
    col_hi = col_matrix.astype(jnp.bfloat16)
    col_lo = (col_matrix - col_hi.astype(jnp.float32)).astype(jnp.bfloat16)
    flat = summed.reshape(local_rows * comps, cols_all)
    by_cols = jnp.dot(flat, col_hi, preferred_element_type=jnp.float32) + jnp.dot(
        flat, col_lo, preferred_element_type=jnp.float32
    )
    by_cols = by_cols.reshape(local_rows, comps * col_tiles * ctrl_cols)

    assert local_rows == tile_rows
    row_blocks = window_blocks(smoothed_basis(filter_taps, basis_rows), tile_rows)[::-1]
    row_matrix = row_blocks.transpose(0, 2, 1).reshape(3 * ctrl_rows, local_rows)
    parts = jnp.dot(row_matrix, by_cols, precision=lax.Precision.HIGHEST)
    parts = parts.reshape(3, ctrl_rows, comps, col_tiles, ctrl_cols)
    parts = parts.transpose(0, 3, 2, 1, 4).reshape(3 * col_tiles, comps * ctrl_rows * ctrl_cols)

    tile_of_box = jnp.zeros((slots,), jnp.int32).at[box_table[:, 0]].set(
        jnp.arange(slots, dtype=jnp.int32)
    )
    tile_of_slot = tile_of_box[owner_perm]
    here = lax.axis_index("tile")
    rel_row = tile_of_slot // col_tiles - here + 1
    pick = rel_row * col_tiles + tile_of_slot % col_tiles
    mine = (rel_row >= 0) & (rel_row <= 2)
    outgoing = jnp.where(mine[:, None], parts[jnp.clip(pick, 0, 3 * col_tiles - 1)], 0.0)
    incoming = lax.all_to_all(outgoing, ("grp", "tile"), 0, 0, tiled=True)
    return jnp.sum(incoming, axis=0).reshape(1, comps, ctrl_rows * ctrl_cols)


def solution(mesh):
    placed = (P("grp", "tile", None, None), P("grp"), P(), P(), P(), P(), P())
    return jax.shard_map(
        local, mesh=mesh, in_specs=placed, out_specs=P(("grp", "tile"), None, None), check_vma=False
    )
```

```python
import jax
import jax.numpy as jnp
from jax import lax
from jax.sharding import PartitionSpec as P


def smoothed_basis(filter_taps, basis):
    reach = filter_taps.shape[0] - 1
    lines = basis.astype(jnp.float32).T[:, None, :]
    kernel = filter_taps.astype(jnp.float32)[::-1][None, None, :]
    full = lax.conv_general_dilated(
        lines, kernel, (1,), [(reach, reach)], precision=lax.Precision.HIGHEST
    )
    return full[:, 0, :].T


def window_blocks(extended, length):
    half = (extended.shape[0] - length) // 2
    padded = jnp.pad(extended, ((length - half, length - half), (0, 0)))
    return padded.reshape(3, length, -1)


def local(sensitivity, inst_weight, filter_taps, basis_rows, basis_cols, box_table, owner_perm):
    tile_rows, ctrl_rows = basis_rows.shape
    tile_cols, ctrl_cols = basis_cols.shape
    local_rows = sensitivity.shape[1]
    cols_all = sensitivity.shape[3]
    col_tiles = cols_all // tile_cols
    comps = sensitivity.shape[2]
    slots = owner_perm.shape[0]

    summed = jnp.sum(
        sensitivity.astype(jnp.float32) * inst_weight[:, None, None, None], axis=0
    ).astype(jnp.bfloat16)

    col_blocks = window_blocks(smoothed_basis(filter_taps, basis_cols), tile_cols)
    col_shift = (
        jnp.arange(col_tiles, dtype=jnp.int32)[:, None]
        - jnp.arange(col_tiles, dtype=jnp.int32)[None, :]
        + 1
    )
    col_valid = (col_shift >= 0) & (col_shift <= 2)
    col_matrix = jnp.where(
        col_valid[:, None, :, None],
        col_blocks[jnp.clip(col_shift, 0, 2)].transpose(0, 2, 1, 3),
        0.0,
    ).reshape(cols_all, col_tiles * ctrl_cols)
    col_hi = col_matrix.astype(jnp.bfloat16)
    col_lo = (col_matrix - col_hi.astype(jnp.float32)).astype(jnp.bfloat16)
    flat = summed.reshape(local_rows * comps, cols_all)
    by_cols = jnp.dot(flat, col_hi, preferred_element_type=jnp.float32) + jnp.dot(
        flat, col_lo, preferred_element_type=jnp.float32
    )
    by_cols = by_cols.reshape(local_rows, comps * col_tiles * ctrl_cols)

    assert local_rows == tile_rows
    row_blocks = window_blocks(smoothed_basis(filter_taps, basis_rows), tile_rows)[::-1]
    row_matrix = row_blocks.transpose(0, 2, 1).reshape(3 * ctrl_rows, local_rows)
    parts = jnp.dot(row_matrix, by_cols, precision=lax.Precision.HIGHEST)
    parts = parts.reshape(3, ctrl_rows, comps, col_tiles, ctrl_cols)
    parts = parts.transpose(0, 3, 2, 1, 4).reshape(3 * col_tiles, comps * ctrl_rows * ctrl_cols)

    tiles = jnp.arange(box_table.shape[0], dtype=jnp.int32)
    tile_of_slot = jnp.sum(
        jnp.where(box_table[:, 0][None, :] == owner_perm[:, None], tiles[None, :], 0), axis=1
    )
    here = lax.axis_index("tile")
    rel_row = tile_of_slot // col_tiles - here + 1
    pick = rel_row * col_tiles + tile_of_slot % col_tiles
    mine = (rel_row >= 0) & (rel_row <= 2)
    outgoing = jnp.where(mine[:, None], parts[jnp.clip(pick, 0, 3 * col_tiles - 1)], 0.0)
    incoming = lax.all_to_all(outgoing, ("grp", "tile"), 0, 0, tiled=True)
    return jnp.sum(incoming, axis=0).reshape(1, comps, ctrl_rows * ctrl_cols)


def solution(mesh):
    placed = (P("grp", "tile", None, None), P("grp"), P(), P(), P(), P(), P())
    return jax.shard_map(
        local, mesh=mesh, in_specs=placed, out_specs=P(("grp", "tile"), None, None), check_vma=False
    )
```

```python
import jax
import jax.numpy as jnp
from jax import lax
from jax.sharding import PartitionSpec as P


def smoothed_bases(filter_taps, bases):
    reach = filter_taps.shape[0] - 1
    lines = jnp.concatenate([b.T for b in bases], axis=0)[:, None, :]
    kernel = filter_taps[::-1][None, None, :]
    full = lax.conv_general_dilated(
        lines, kernel, (1,), [(reach, reach)], preferred_element_type=jnp.float32
    )[:, 0, :].T
    sizes = [b.shape[1] for b in bases]
    return [full[:, sum(sizes[:i]) : sum(sizes[: i + 1])] for i in range(len(bases))]


def window_blocks(extended, length):
    half = (extended.shape[0] - length) // 2
    padded = jnp.pad(extended, ((length - half, length - half), (0, 0)))
    return padded.reshape(3, length, -1)


def local(sensitivity, inst_weight, filter_taps, basis_rows, basis_cols, box_table, owner_perm):
    tile_rows, ctrl_rows = basis_rows.shape
    tile_cols, ctrl_cols = basis_cols.shape
    local_rows = sensitivity.shape[1]
    cols_all = sensitivity.shape[3]
    col_tiles = cols_all // tile_cols
    comps = sensitivity.shape[2]
    slots = owner_perm.shape[0]

    summed = jnp.sum(
        sensitivity.astype(jnp.float32) * inst_weight[:, None, None, None], axis=0
    ).astype(jnp.bfloat16)

    row_ext, col_ext = smoothed_bases(filter_taps, (basis_rows, basis_cols))
    col_blocks = window_blocks(col_ext, tile_cols)
    col_shift = (
        jnp.arange(col_tiles, dtype=jnp.int32)[:, None]
        - jnp.arange(col_tiles, dtype=jnp.int32)[None, :]
        + 1
    )
    col_valid = (col_shift >= 0) & (col_shift <= 2)
    col_matrix = jnp.where(
        col_valid[:, None, :, None],
        col_blocks[jnp.clip(col_shift, 0, 2)].transpose(0, 2, 1, 3),
        0.0,
    ).reshape(cols_all, col_tiles * ctrl_cols)
    col_hi = col_matrix.astype(jnp.bfloat16)
    col_lo = (col_matrix - col_hi.astype(jnp.float32)).astype(jnp.bfloat16)
    by_cols = jnp.einsum("rkc,cn->rkn", summed, col_hi, preferred_element_type=jnp.float32)
    by_cols = by_cols + jnp.einsum(
        "rkc,cn->rkn", summed, col_lo, preferred_element_type=jnp.float32
    )
    by_cols = by_cols.reshape(local_rows, comps * col_tiles * ctrl_cols)

    assert local_rows == tile_rows
    row_blocks = window_blocks(row_ext, tile_rows)[::-1]
    row_matrix = row_blocks.transpose(0, 2, 1).reshape(3 * ctrl_rows, local_rows)
    parts = jnp.dot(row_matrix, by_cols, precision=lax.Precision.HIGHEST)
    parts = parts.reshape(3, ctrl_rows, comps, col_tiles, ctrl_cols)
    parts = parts.transpose(0, 3, 2, 1, 4).reshape(3 * col_tiles, comps * ctrl_rows * ctrl_cols)

    tiles = jnp.arange(box_table.shape[0], dtype=jnp.int32)
    tile_of_slot = jnp.sum(
        jnp.where(box_table[:, 0][None, :] == owner_perm[:, None], tiles[None, :], 0), axis=1
    )
    here = lax.axis_index("tile")
    rel_row = tile_of_slot // col_tiles - here + 1
    pick = rel_row * col_tiles + tile_of_slot % col_tiles
    mine = (rel_row >= 0) & (rel_row <= 2)
    outgoing = jnp.where(mine[:, None], parts[jnp.clip(pick, 0, 3 * col_tiles - 1)], 0.0)
    outgoing = outgoing.astype(jnp.bfloat16).reshape(slots, comps * ctrl_rows * ctrl_cols)
    incoming = lax.all_to_all(outgoing, ("grp", "tile"), 0, 0, tiled=True)
    total = jnp.sum(incoming.astype(jnp.float32), axis=0)
    return total.reshape(1, comps, ctrl_rows * ctrl_cols)


def solution(mesh):
    placed = (P("grp", "tile", None, None), P("grp"), P(), P(), P(), P(), P())
    return jax.shard_map(
        local, mesh=mesh, in_specs=placed, out_specs=P(("grp", "tile"), None, None), check_vma=False
    )
```

```python
import functools

import jax
import jax.numpy as jnp
from jax import lax
from jax.experimental import pallas as pl
from jax.experimental.pallas import tpu as pltpu
from jax.sharding import PartitionSpec as P


def fold_kernel(half, w_ref, taps_ref, bases_ref, sens_ref, out_ref, ct_ref):
    insts, comps, rows, cols = sens_ref.shape
    ctrl = bases_ref.shape[0] // 2
    tile = bases_ref.shape[1]
    col_tiles = cols // tile
    period = taps_ref.shape[1]

    base = jnp.broadcast_to(taps_ref[...], (tile, period))
    blocks = []
    for b in range(3):
        rolled = pltpu.roll(base, (-(tile * (b - 1) + half)) % period, 1, stride=1, stride_axis=0)
        blocks.append(rolled[:, :tile])
    toeplitz = jnp.concatenate(blocks, axis=1).astype(jnp.bfloat16)
    smoothed = jnp.dot(bases_ref[...], toeplitz, preferred_element_type=jnp.float32)

    ct_ref[...] = jnp.zeros(ct_ref.shape, jnp.float32)
    for y in range(col_tiles):
        for cb in range(max(0, y - 1), min(col_tiles, y + 2)):
            b = cb - y + 1
            ct_ref[ctrl * y : ctrl * (y + 1), tile * cb : tile * (cb + 1)] = smoothed[
                :ctrl, tile * b : tile * (b + 1)
            ]
    ct = ct_ref[...]
    ct_hi = ct.astype(jnp.bfloat16)
    ct_lo = (ct - ct_hi.astype(jnp.float32)).astype(jnp.bfloat16)
    rows_matrix = jnp.concatenate(
        [smoothed[ctrl:, tile * (2 - d) : tile * (3 - d)] for d in range(3)], axis=0
    )
    nt = (((1,), (1,)), ((), ()))
    for k in range(comps):
        summed = (sens_ref[0, k].astype(jnp.float32) * w_ref[0]).astype(jnp.float32)
        for i in range(1, insts):
            summed = summed + sens_ref[i, k].astype(jnp.float32) * w_ref[i]
        summed = summed.astype(jnp.bfloat16)
        by_cols = lax.dot_general(summed, ct_hi, nt, preferred_element_type=jnp.float32)
        by_cols = by_cols + lax.dot_general(summed, ct_lo, nt, preferred_element_type=jnp.float32)
        out_ref[k] = jnp.dot(
            rows_matrix, by_cols, precision=lax.Precision.HIGHEST, preferred_element_type=jnp.float32
        )


def local(sensitivity, inst_weight, filter_taps, basis_rows, basis_cols, box_table, owner_perm):
    tile_rows, ctrl_rows = basis_rows.shape
    tile_cols, ctrl_cols = basis_cols.shape
    insts, local_rows, comps, cols_all = sensitivity.shape
    col_tiles = cols_all // tile_cols
    slots = owner_perm.shape[0]
    assert local_rows == tile_rows and tile_rows == tile_cols and ctrl_rows == ctrl_cols

    period = 4 * tile_rows
    taps_row = jnp.pad(filter_taps.astype(jnp.float32), (0, period - filter_taps.shape[0]))[None, :]
    bases = jnp.concatenate([basis_cols.T, basis_rows.T], axis=0)
    parts = pl.pallas_call(
        functools.partial(fold_kernel, (filter_taps.shape[0] - 1) // 2),
        out_shape=jax.ShapeDtypeStruct((comps, 3 * ctrl_rows, col_tiles * ctrl_cols), jnp.float32),
        in_specs=[
            pl.BlockSpec(memory_space=pltpu.SMEM),
            pl.BlockSpec(memory_space=pltpu.VMEM),
            pl.BlockSpec(memory_space=pltpu.VMEM),
            pl.BlockSpec(memory_space=pltpu.VMEM),
        ],
        out_specs=pl.BlockSpec(memory_space=pltpu.VMEM),
        scratch_shapes=[pltpu.VMEM((col_tiles * ctrl_cols, cols_all), jnp.float32)],
    )(inst_weight, taps_row, bases, jnp.transpose(sensitivity, (0, 2, 1, 3)))
    parts = parts.reshape(comps, 3, ctrl_rows, col_tiles, ctrl_cols)
    parts = parts.transpose(1, 3, 0, 2, 4).reshape(3 * col_tiles, comps * ctrl_rows * ctrl_cols)

    tiles = jnp.arange(box_table.shape[0], dtype=jnp.int32)
    tile_of_slot = jnp.sum(
        jnp.where(box_table[:, 0][None, :] == owner_perm[:, None], tiles[None, :], 0), axis=1
    )
    here = lax.axis_index("tile")
    rel_row = tile_of_slot // col_tiles - here + 1
    pick = rel_row * col_tiles + tile_of_slot % col_tiles
    mine = (rel_row >= 0) & (rel_row <= 2)
    outgoing = jnp.where(mine[:, None], parts[jnp.clip(pick, 0, 3 * col_tiles - 1)], 0.0)
    outgoing = outgoing.astype(jnp.bfloat16)
    incoming = lax.all_to_all(outgoing, ("grp", "tile"), 0, 0, tiled=True)
    total = jnp.sum(incoming.astype(jnp.float32), axis=0)
    return total.reshape(1, comps, ctrl_rows * ctrl_cols)


def solution(mesh):
    placed = (P("grp", "tile", None, None), P("grp"), P(), P(), P(), P(), P())
    return jax.shard_map(
        local, mesh=mesh, in_specs=placed, out_specs=P(("grp", "tile"), None, None), check_vma=False
    )
```

```python
import functools

import jax
import jax.numpy as jnp
from jax import lax
from jax.experimental import pallas as pl
from jax.experimental.pallas import tpu as pltpu
from jax.sharding import PartitionSpec as P


def fold_kernel(w_ref, taps_ref, cols_ref, rows_ref, sens_ref, out_ref, ct_ref, taps_row):
    insts, comps, rows, cols = sens_ref.shape
    ctrl, tile = cols_ref.shape
    col_tiles = cols // tile
    period = taps_row.shape[1]
    half = (taps_ref.shape[1] - 1) // 2

    taps_row[...] = jnp.zeros(taps_row.shape, jnp.float32)
    taps_row[:, : taps_ref.shape[1]] = taps_ref[...].astype(jnp.float32)
    base = jnp.broadcast_to(taps_row[...], (tile, period))
    blocks = []
    for b in range(3):
        rolled = pltpu.roll(base, (-(tile * (b - 1) + half)) % period, 1, stride=1, stride_axis=0)
        blocks.append(rolled[:, :tile])
    toeplitz = jnp.concatenate(blocks, axis=1).astype(jnp.bfloat16)
    bases = jnp.concatenate([cols_ref[...], rows_ref[...]], axis=0)
    smoothed = jnp.dot(bases, toeplitz, preferred_element_type=jnp.float32)

    ct_ref[...] = jnp.zeros(ct_ref.shape, jnp.float32)
    for y in range(col_tiles):
        for cb in range(max(0, y - 1), min(col_tiles, y + 2)):
            b = cb - y + 1
            ct_ref[ctrl * y : ctrl * (y + 1), tile * cb : tile * (cb + 1)] = smoothed[
                :ctrl, tile * b : tile * (b + 1)
            ]
    ct = ct_ref[...]
    ct_hi = ct.astype(jnp.bfloat16)
    ct_lo = (ct - ct_hi.astype(jnp.float32)).astype(jnp.bfloat16)
    rows_matrix = jnp.concatenate(
        [smoothed[ctrl:, tile * (2 - d) : tile * (3 - d)] for d in range(3)], axis=0
    )
    nt = (((1,), (1,)), ((), ()))
    for k in range(comps):
        summed = (sens_ref[0, k].astype(jnp.float32) * w_ref[0]).astype(jnp.float32)
        for i in range(1, insts):
            summed = summed + sens_ref[i, k].astype(jnp.float32) * w_ref[i]
        summed = summed.astype(jnp.bfloat16)
        by_cols = lax.dot_general(summed, ct_hi, nt, preferred_element_type=jnp.float32)
        by_cols = by_cols + lax.dot_general(summed, ct_lo, nt, preferred_element_type=jnp.float32)
        out_ref[k] = jnp.dot(
            rows_matrix, by_cols, precision=lax.Precision.HIGHEST, preferred_element_type=jnp.float32
        ).astype(out_ref.dtype)


def local(sensitivity, inst_weight, filter_taps, basis_rows, basis_cols, box_table, owner_perm):
    tile_rows, ctrl_rows = basis_rows.shape
    tile_cols, ctrl_cols = basis_cols.shape
    insts, local_rows, comps, cols_all = sensitivity.shape
    col_tiles = cols_all // tile_cols
    slots = owner_perm.shape[0]
    assert local_rows == tile_rows and tile_rows == tile_cols and ctrl_rows == ctrl_cols

    period = 4 * tile_rows
    parts = pl.pallas_call(
        fold_kernel,
        out_shape=jax.ShapeDtypeStruct((comps, 3 * ctrl_rows, col_tiles * ctrl_cols), jnp.bfloat16),
        in_specs=[pl.BlockSpec(memory_space=pltpu.SMEM)] + [pl.BlockSpec(memory_space=pltpu.VMEM)] * 4,
        out_specs=pl.BlockSpec(memory_space=pltpu.VMEM),
        scratch_shapes=[
            pltpu.VMEM((col_tiles * ctrl_cols, cols_all), jnp.float32),
            pltpu.VMEM((1, period), jnp.float32),
        ],
    )(
        inst_weight,
        filter_taps[None, :],
        basis_cols.T,
        basis_rows.T,
        jnp.transpose(sensitivity, (0, 2, 1, 3)),
    )
    parts = parts.reshape(comps, 3, ctrl_rows, col_tiles, ctrl_cols)
    parts = parts.transpose(1, 3, 0, 2, 4).reshape(3 * col_tiles, comps * ctrl_rows * ctrl_cols)

    tiles = jnp.arange(box_table.shape[0], dtype=jnp.int32)
    tile_of_slot = jnp.sum(
        jnp.where(box_table[:, 0][None, :] == owner_perm[:, None], tiles[None, :], 0), axis=1
    )
    here = lax.axis_index("tile")
    rel_row = tile_of_slot // col_tiles - here + 1
    pick = rel_row * col_tiles + tile_of_slot % col_tiles
    select = (pick[:, None] == jnp.arange(3 * col_tiles, dtype=jnp.int32)[None, :]).astype(
        jnp.bfloat16
    )
    outgoing = jnp.dot(select, parts, preferred_element_type=jnp.float32).astype(jnp.bfloat16)
    incoming = lax.all_to_all(outgoing, ("grp", "tile"), 0, 0, tiled=True)
    total = jnp.sum(
        incoming.astype(jnp.float32).reshape(slots, comps, ctrl_rows * ctrl_cols), axis=0
    )
    return total[None]


def solution(mesh):
    placed = (P("grp", "tile", None, None), P("grp"), P(), P(), P(), P(), P())
    return jax.shard_map(
        local, mesh=mesh, in_specs=placed, out_specs=P(("grp", "tile"), None, None), check_vma=False
    )
```

```python
import functools

import jax
import jax.numpy as jnp
from jax import lax
from jax.experimental import pallas as pl
from jax.experimental.pallas import tpu as pltpu
from jax.sharding import PartitionSpec as P


def fold_kernel(
    w_ref, taps_ref, cols_ref, rows_ref, sens_ref, pick_ref, out_ref, ct_ref, taps_row, parts_ref
):
    insts, comps, rows, cols = sens_ref.shape
    ctrl, tile = cols_ref.shape
    col_tiles = cols // tile
    period = taps_row.shape[1]
    half = (taps_ref.shape[0] - 1) // 2

    taps_row[...] = jnp.zeros(taps_row.shape, jnp.float32)
    taps_row[:, : taps_ref.shape[0]] = taps_ref[...].astype(jnp.float32)[None, :]
    base = jnp.broadcast_to(taps_row[...], (tile, period))
    blocks = []
    for b in range(3):
        rolled = pltpu.roll(base, (-(tile * (b - 1) + half)) % period, 1, stride=1, stride_axis=0)
        blocks.append(rolled[:, :tile])
    toeplitz = jnp.concatenate(blocks, axis=1).astype(jnp.bfloat16)
    bases = jnp.concatenate([cols_ref[...], rows_ref[...]], axis=0)
    smoothed = jnp.dot(bases, toeplitz, preferred_element_type=jnp.float32)

    ct_ref[...] = jnp.zeros(ct_ref.shape, jnp.float32)
    for y in range(col_tiles):
        for cb in range(max(0, y - 1), min(col_tiles, y + 2)):
            b = cb - y + 1
            ct_ref[ctrl * y : ctrl * (y + 1), tile * cb : tile * (cb + 1)] = smoothed[
                :ctrl, tile * b : tile * (b + 1)
            ]
    ct = ct_ref[...]
    ct_hi = ct.astype(jnp.bfloat16)
    ct_lo = (ct - ct_hi.astype(jnp.float32)).astype(jnp.bfloat16)
    rows_matrix = jnp.concatenate(
        [smoothed[ctrl:, tile * (2 - d) : tile * (3 - d)] for d in range(3)], axis=0
    )
    nt = (((1,), (1,)), ((), ()))
    lanes = col_tiles * ctrl
    block = ctrl * ctrl
    spread = (
        lax.broadcasted_iota(jnp.int32, (3 * ctrl, 3 * block), 0)
        == lax.broadcasted_iota(jnp.int32, (3 * ctrl, 3 * block), 1) // ctrl
    ).astype(jnp.bfloat16)
    keep = (
        lax.broadcasted_iota(jnp.int32, (lanes, 3 * block), 0) % ctrl
        == lax.broadcasted_iota(jnp.int32, (lanes, 3 * block), 1) % ctrl
    )
    gather_y = (
        lax.broadcasted_iota(jnp.int32, (col_tiles, lanes), 0)
        == lax.broadcasted_iota(jnp.int32, (col_tiles, lanes), 1) // ctrl
    ).astype(jnp.bfloat16)
    for k in range(comps):
        summed = (sens_ref[0, k].astype(jnp.float32) * w_ref[0]).astype(jnp.float32)
        for i in range(1, insts):
            summed = summed + sens_ref[i, k].astype(jnp.float32) * w_ref[i]
        summed = summed.astype(jnp.bfloat16)
        by_cols = lax.dot_general(summed, ct_hi, nt, preferred_element_type=jnp.float32)
        by_cols = by_cols + lax.dot_general(summed, ct_lo, nt, preferred_element_type=jnp.float32)
        z = jnp.dot(
            rows_matrix, by_cols, precision=lax.Precision.HIGHEST, preferred_element_type=jnp.float32
        )
        zt = z.T.astype(jnp.bfloat16)
        wide = jnp.dot(zt, spread, preferred_element_type=jnp.float32)
        wide = jnp.where(keep, wide, 0.0).astype(jnp.bfloat16)
        moved = jnp.dot(gather_y, wide, preferred_element_type=jnp.float32).astype(jnp.bfloat16)
        for d in range(3):
            parts_ref[col_tiles * d : col_tiles * (d + 1), block * k : block * (k + 1)] = moved[
                :, block * d : block * (d + 1)
            ]
    rows_of_parts = parts_ref.shape[0]
    select = (
        pick_ref[...] == lax.broadcasted_iota(jnp.int32, (out_ref.shape[0], rows_of_parts), 1)
    ).astype(jnp.bfloat16)
    out_ref[...] = jnp.dot(select, parts_ref[...], preferred_element_type=jnp.float32).astype(
        out_ref.dtype
    )


def local(sensitivity, inst_weight, filter_taps, basis_rows, basis_cols, box_table, owner_perm):
    tile_rows, ctrl_rows = basis_rows.shape
    tile_cols, ctrl_cols = basis_cols.shape
    insts, local_rows, comps, cols_all = sensitivity.shape
    col_tiles = cols_all // tile_cols
    slots = owner_perm.shape[0]
    assert local_rows == tile_rows and tile_rows == tile_cols and ctrl_rows == ctrl_cols

    period = 4 * tile_rows
    tiles = jnp.arange(box_table.shape[0], dtype=jnp.int32)
    tile_of_slot = jnp.sum(
        jnp.where(box_table[:, 0][None, :] == owner_perm[:, None], tiles[None, :], 0),
        axis=1,
        keepdims=True,
    )
    here = lax.axis_index("tile")
    rel_row = tile_of_slot // col_tiles - here + 1
    pick = rel_row * col_tiles + tile_of_slot % col_tiles
    outgoing = pl.pallas_call(
        fold_kernel,
        out_shape=jax.ShapeDtypeStruct((slots, comps * ctrl_rows * ctrl_cols), jnp.bfloat16),
        in_specs=[pl.BlockSpec(memory_space=pltpu.SMEM)] + [pl.BlockSpec(memory_space=pltpu.VMEM)] * 5,
        out_specs=pl.BlockSpec(memory_space=pltpu.VMEM),
        scratch_shapes=[
            pltpu.VMEM((col_tiles * ctrl_cols, cols_all), jnp.float32),
            pltpu.VMEM((1, period), jnp.float32),
            pltpu.VMEM((3 * col_tiles, comps * ctrl_rows * ctrl_cols), jnp.bfloat16),
        ],
    )(
        inst_weight,
        filter_taps,
        basis_cols.T,
        basis_rows.T,
        jnp.transpose(sensitivity, (0, 2, 1, 3)),
        pick,
    )
    incoming = lax.all_to_all(outgoing, ("grp", "tile"), 0, 0, tiled=True)
    total = jnp.sum(
        incoming.astype(jnp.float32).reshape(slots, comps, ctrl_rows * ctrl_cols), axis=0
    )
    return total[None]


def solution(mesh):
    placed = (P("grp", "tile", None, None), P("grp"), P(), P(), P(), P(), P())
    return jax.shard_map(
        local, mesh=mesh, in_specs=placed, out_specs=P(("grp", "tile"), None, None), check_vma=False
    )
```

```python
import functools

import jax
import jax.numpy as jnp
from jax import lax
from jax.experimental import pallas as pl
from jax.experimental.pallas import tpu as pltpu
from jax.sharding import PartitionSpec as P


def fold_kernel(w_ref, taps_ref, cols_ref, rows_ref, sens_ref, out_ref, ct_ref, taps_row):
    insts, comps, rows, cols = sens_ref.shape
    ctrl, tile = cols_ref.shape
    col_tiles = cols // tile
    period = taps_row.shape[1]
    half = (taps_ref.shape[0] - 1) // 2

    taps_row[...] = jnp.zeros(taps_row.shape, jnp.float32)
    taps_row[:, : taps_ref.shape[0]] = taps_ref[...].astype(jnp.float32)[None, :]
    base = jnp.broadcast_to(taps_row[...], (tile, period))
    blocks = []
    for b in range(3):
        rolled = pltpu.roll(base, (-(tile * (b - 1) + half)) % period, 1, stride=1, stride_axis=0)
        blocks.append(rolled[:, :tile])
    toeplitz = jnp.concatenate(blocks, axis=1).astype(jnp.bfloat16)
    bases = jnp.concatenate([cols_ref[...], rows_ref[...]], axis=0)
    smoothed = jnp.dot(bases, toeplitz, preferred_element_type=jnp.float32)

    ct_ref[...] = jnp.zeros(ct_ref.shape, jnp.float32)
    for y in range(col_tiles):
        for cb in range(max(0, y - 1), min(col_tiles, y + 2)):
            b = cb - y + 1
            ct_ref[ctrl * y : ctrl * (y + 1), tile * cb : tile * (cb + 1)] = smoothed[
                :ctrl, tile * b : tile * (b + 1)
            ]
    ct = ct_ref[...]
    ct_hi = ct.astype(jnp.bfloat16)
    ct_lo = (ct - ct_hi.astype(jnp.float32)).astype(jnp.bfloat16)
    rows_matrix = jnp.concatenate(
        [smoothed[ctrl:, tile * (2 - d) : tile * (3 - d)] for d in range(3)], axis=0
    )
    nt = (((1,), (1,)), ((), ()))
    for k in range(comps):
        summed = (sens_ref[0, k].astype(jnp.float32) * w_ref[0]).astype(jnp.float32)
        for i in range(1, insts):
            summed = summed + sens_ref[i, k].astype(jnp.float32) * w_ref[i]
        summed = summed.astype(jnp.bfloat16)
        by_cols = lax.dot_general(summed, ct_hi, nt, preferred_element_type=jnp.float32)
        by_cols = by_cols + lax.dot_general(summed, ct_lo, nt, preferred_element_type=jnp.float32)
        out_ref[k] = jnp.dot(
            rows_matrix, by_cols, precision=lax.Precision.HIGHEST, preferred_element_type=jnp.float32
        ).astype(out_ref.dtype)


def local(sensitivity, inst_weight, filter_taps, basis_rows, basis_cols, box_table, owner_perm):
    tile_rows, ctrl_rows = basis_rows.shape
    tile_cols, ctrl_cols = basis_cols.shape
    insts, local_rows, comps, cols_all = sensitivity.shape
    col_tiles = cols_all // tile_cols
    slots = owner_perm.shape[0]
    assert local_rows == tile_rows and tile_rows == tile_cols and ctrl_rows == ctrl_cols

    period = 4 * tile_rows
    parts = pl.pallas_call(
        fold_kernel,
        out_shape=jax.ShapeDtypeStruct((comps, 3 * ctrl_rows, col_tiles * ctrl_cols), jnp.bfloat16),
        in_specs=[pl.BlockSpec(memory_space=pltpu.SMEM)] + [pl.BlockSpec(memory_space=pltpu.VMEM)] * 4,
        out_specs=pl.BlockSpec(memory_space=pltpu.VMEM),
        scratch_shapes=[
            pltpu.VMEM((col_tiles * ctrl_cols, cols_all), jnp.float32),
            pltpu.VMEM((1, period), jnp.float32),
        ],
    )(
        inst_weight,
        filter_taps,
        basis_cols.T,
        basis_rows.T,
        jnp.transpose(sensitivity, (0, 2, 1, 3)),
    )
    parts = parts.reshape(comps, 3, ctrl_rows, col_tiles, ctrl_cols)
    parts = parts.transpose(1, 3, 0, 2, 4).reshape(3 * col_tiles, comps * ctrl_rows * ctrl_cols)

    tiles = jnp.arange(box_table.shape[0], dtype=jnp.int32)
    tile_of_slot = jnp.sum(
        jnp.where(box_table[:, 0][None, :] == owner_perm[:, None], tiles[None, :], 0), axis=1
    )
    here = lax.axis_index("tile")
    rel_row = tile_of_slot // col_tiles - here + 1
    pick = rel_row * col_tiles + tile_of_slot % col_tiles
    select = (pick[:, None] == jnp.arange(3 * col_tiles, dtype=jnp.int32)[None, :]).astype(
        jnp.bfloat16
    )
    outgoing = jnp.dot(select, parts, preferred_element_type=jnp.float32).astype(jnp.bfloat16)
    incoming = lax.all_to_all(outgoing, ("grp", "tile"), 0, 0, tiled=True)
    total = jnp.sum(
        incoming.astype(jnp.float32).reshape(slots, comps, ctrl_rows * ctrl_cols), axis=0
    )
    return total[None]


def solution(mesh):
    placed = (P("grp", "tile", None, None), P("grp"), P(), P(), P(), P(), P())
    return jax.shard_map(
        local, mesh=mesh, in_specs=placed, out_specs=P(("grp", "tile"), None, None), check_vma=False
    )
```

```python
import functools

import jax
import jax.numpy as jnp
from jax import lax
from jax.experimental import pallas as pl
from jax.experimental.pallas import tpu as pltpu
from jax.sharding import PartitionSpec as P


def fold_kernel(w_ref, taps_ref, cols_ref, rows_ref, sens_ref, out_ref, ct_ref, taps_row):
    insts, comps, rows, cols = sens_ref.shape
    ctrl, tile = cols_ref.shape
    col_tiles = cols // tile
    period = taps_row.shape[1]
    half = (taps_ref.shape[0] - 1) // 2

    taps_row[...] = jnp.zeros(taps_row.shape, jnp.float32)
    taps_row[:, : taps_ref.shape[0]] = taps_ref[...].astype(jnp.float32)[None, :]
    base = jnp.broadcast_to(taps_row[...], (tile, period))
    blocks = []
    for b in range(3):
        rolled = pltpu.roll(base, (-(tile * (b - 1) + half)) % period, 1, stride=1, stride_axis=0)
        blocks.append(rolled[:, :tile])
    toeplitz = jnp.concatenate(blocks, axis=1).astype(jnp.bfloat16)
    bases = jnp.concatenate([cols_ref[...], rows_ref[...]], axis=0)
    smoothed = jnp.dot(bases, toeplitz, preferred_element_type=jnp.float32)

    ct_ref[...] = jnp.zeros(ct_ref.shape, jnp.float32)
    for y in range(col_tiles):
        for cb in range(max(0, y - 1), min(col_tiles, y + 2)):
            b = cb - y + 1
            ct_ref[ctrl * y : ctrl * (y + 1), tile * cb : tile * (cb + 1)] = smoothed[
                :ctrl, tile * b : tile * (b + 1)
            ]
    ct = ct_ref[...]
    ct_hi = ct.astype(jnp.bfloat16)
    ct_lo = (ct - ct_hi.astype(jnp.float32)).astype(jnp.bfloat16)
    rows_matrix = jnp.concatenate(
        [smoothed[ctrl:, tile * (2 - d) : tile * (3 - d)] for d in range(3)], axis=0
    )
    nt = (((1,), (1,)), ((), ()))
    for k in range(comps):
        summed = (sens_ref[0, k].astype(jnp.float32) * w_ref[0]).astype(jnp.float32)
        for i in range(1, insts):
            summed = summed + sens_ref[i, k].astype(jnp.float32) * w_ref[i]
        summed = summed.astype(jnp.bfloat16)
        by_cols = lax.dot_general(summed, ct_hi, nt, preferred_element_type=jnp.float32)
        by_cols = by_cols + lax.dot_general(summed, ct_lo, nt, preferred_element_type=jnp.float32)
        out_ref[k] = jnp.dot(
            rows_matrix, by_cols, precision=lax.Precision.HIGHEST, preferred_element_type=jnp.float32
        ).astype(out_ref.dtype)


def local(sensitivity, inst_weight, filter_taps, basis_rows, basis_cols, box_table, owner_perm):
    tile_rows, ctrl_rows = basis_rows.shape
    tile_cols, ctrl_cols = basis_cols.shape
    insts, local_rows, comps, cols_all = sensitivity.shape
    col_tiles = cols_all // tile_cols
    slots = owner_perm.shape[0]
    assert local_rows == tile_rows and tile_rows == tile_cols and ctrl_rows == ctrl_cols

    period = 4 * tile_rows
    parts = pl.pallas_call(
        fold_kernel,
        out_shape=jax.ShapeDtypeStruct((comps, 3 * ctrl_rows, col_tiles * ctrl_cols), jnp.bfloat16),
        in_specs=[pl.BlockSpec(memory_space=pltpu.SMEM)] + [pl.BlockSpec(memory_space=pltpu.VMEM)] * 4,
        out_specs=pl.BlockSpec(memory_space=pltpu.VMEM),
        scratch_shapes=[
            pltpu.VMEM((col_tiles * ctrl_cols, cols_all), jnp.float32),
            pltpu.VMEM((1, period), jnp.float32),
        ],
    )(
        inst_weight,
        filter_taps,
        basis_cols.T,
        basis_rows.T,
        jnp.transpose(sensitivity, (0, 2, 1, 3)),
    )
    parts = parts.reshape(comps, 3, ctrl_rows, col_tiles, ctrl_cols)
    parts = parts.transpose(1, 3, 0, 2, 4).reshape(3 * col_tiles, comps * ctrl_rows * ctrl_cols)

    tiles = jnp.arange(box_table.shape[0], dtype=jnp.int32)
    tile_of_slot = jnp.sum(
        jnp.where(box_table[:, 0][None, :] == owner_perm[:, None], tiles[None, :], 0), axis=1
    )
    here = lax.axis_index("tile")
    rel_row = tile_of_slot // col_tiles - here + 1
    pick = rel_row * col_tiles + tile_of_slot % col_tiles
    select = (pick[:, None] == jnp.arange(3 * col_tiles, dtype=jnp.int32)[None, :]).astype(
        jnp.bfloat16
    )
    outgoing = jnp.einsum(
        "ms,sab->mab", select, parts.reshape(3 * col_tiles, 2, -1), preferred_element_type=jnp.float32
    ).astype(jnp.bfloat16)
    incoming = lax.all_to_all(outgoing, ("grp", "tile"), 0, 0, tiled=True)
    total = jnp.sum(
        incoming.astype(jnp.float32).reshape(slots, 1, comps, ctrl_rows * ctrl_cols), axis=0
    )
    return total


def solution(mesh):
    placed = (P("grp", "tile", None, None), P("grp"), P(), P(), P(), P(), P())
    return jax.shard_map(
        local, mesh=mesh, in_specs=placed, out_specs=P(("grp", "tile"), None, None), check_vma=False
    )
```

```python
import functools

import jax
import jax.numpy as jnp
from jax import lax
from jax.experimental import pallas as pl
from jax.experimental.pallas import tpu as pltpu
from jax.sharding import PartitionSpec as P


def fold_kernel(
    w_ref, taps_ref, cols_ref, rows_ref, sens_ref, out_ref, ct_ref, taps_row, hi_ref, lo_ref, rows_mat
):
    insts, _, rows, cols = sens_ref.shape
    ctrl, tile = cols_ref.shape
    col_tiles = cols // tile
    period = taps_row.shape[1]
    half = (taps_ref.shape[0] - 1) // 2

    @pl.when(pl.program_id(0) == 0)
    def _():
        taps_row[...] = jnp.zeros(taps_row.shape, jnp.float32)
        taps_row[:, : taps_ref.shape[0]] = taps_ref[...].astype(jnp.float32)[None, :]
        base = jnp.broadcast_to(taps_row[...], (tile, period))
        blocks = []
        for b in range(3):
            rolled = pltpu.roll(base, (-(tile * (b - 1) + half)) % period, 1, stride=1, stride_axis=0)
            blocks.append(rolled[:, :tile])
        toeplitz = jnp.concatenate(blocks, axis=1).astype(jnp.bfloat16)
        bases = jnp.concatenate([cols_ref[...], rows_ref[...]], axis=0)
        smoothed = jnp.dot(bases, toeplitz, preferred_element_type=jnp.float32)
        ct_ref[...] = jnp.zeros(ct_ref.shape, jnp.float32)
        for y in range(col_tiles):
            for cb in range(max(0, y - 1), min(col_tiles, y + 2)):
                b = cb - y + 1
                ct_ref[ctrl * y : ctrl * (y + 1), tile * cb : tile * (cb + 1)] = smoothed[
                    :ctrl, tile * b : tile * (b + 1)
                ]
        ct = ct_ref[...]
        ct_hi = ct.astype(jnp.bfloat16)
        hi_ref[...] = ct_hi
        lo_ref[...] = (ct - ct_hi.astype(jnp.float32)).astype(jnp.bfloat16)
        rows_mat[...] = jnp.concatenate(
            [smoothed[ctrl:, tile * (2 - d) : tile * (3 - d)] for d in range(3)], axis=0
        )

    nt = (((1,), (1,)), ((), ()))
    summed = (sens_ref[0, 0].astype(jnp.float32) * w_ref[0]).astype(jnp.float32)
    for i in range(1, insts):
        summed = summed + sens_ref[i, 0].astype(jnp.float32) * w_ref[i]
    summed = summed.astype(jnp.bfloat16)
    by_cols = lax.dot_general(summed, hi_ref[...], nt, preferred_element_type=jnp.float32)
    by_cols = by_cols + lax.dot_general(summed, lo_ref[...], nt, preferred_element_type=jnp.float32)
    out_ref[0] = jnp.dot(
        rows_mat[...], by_cols, precision=lax.Precision.HIGHEST, preferred_element_type=jnp.float32
    ).astype(out_ref.dtype)


def local(sensitivity, inst_weight, filter_taps, basis_rows, basis_cols, box_table, owner_perm):
    tile_rows, ctrl_rows = basis_rows.shape
    tile_cols, ctrl_cols = basis_cols.shape
    insts, local_rows, comps, cols_all = sensitivity.shape
    col_tiles = cols_all // tile_cols
    slots = owner_perm.shape[0]
    assert local_rows == tile_rows and tile_rows == tile_cols and ctrl_rows == ctrl_cols

    period = 4 * tile_rows
    parts = pl.pallas_call(
        fold_kernel,
        out_shape=jax.ShapeDtypeStruct((comps, 3 * ctrl_rows, col_tiles * ctrl_cols), jnp.bfloat16),
        grid=(comps,),
        in_specs=[
            pl.BlockSpec(memory_space=pltpu.SMEM),
            pl.BlockSpec(filter_taps.shape, lambda k: (0,)),
            pl.BlockSpec(basis_cols.T.shape, lambda k: (0, 0)),
            pl.BlockSpec(basis_rows.T.shape, lambda k: (0, 0)),
            pl.BlockSpec((insts, 1, local_rows, cols_all), lambda k: (0, k, 0, 0)),
        ],
        out_specs=pl.BlockSpec((1, 3 * ctrl_rows, col_tiles * ctrl_cols), lambda k: (k, 0, 0)),
        scratch_shapes=[
            pltpu.VMEM((col_tiles * ctrl_cols, cols_all), jnp.float32),
            pltpu.VMEM((1, period), jnp.float32),
            pltpu.VMEM((col_tiles * ctrl_cols, cols_all), jnp.bfloat16),
            pltpu.VMEM((col_tiles * ctrl_cols, cols_all), jnp.bfloat16),
            pltpu.VMEM((3 * ctrl_rows, local_rows), jnp.float32),
        ],
        compiler_params=pltpu.CompilerParams(dimension_semantics=("arbitrary",)),
    )(
        inst_weight,
        filter_taps,
        basis_cols.T,
        basis_rows.T,
        jnp.transpose(sensitivity, (0, 2, 1, 3)),
    )
    parts = parts.reshape(comps, 3, ctrl_rows, col_tiles, ctrl_cols)
    parts = parts.transpose(1, 3, 0, 2, 4).reshape(3 * col_tiles, comps * ctrl_rows * ctrl_cols)

    tiles = jnp.arange(box_table.shape[0], dtype=jnp.int32)
    tile_of_slot = jnp.sum(
        jnp.where(box_table[:, 0][None, :] == owner_perm[:, None], tiles[None, :], 0), axis=1
    )
    here = lax.axis_index("tile")
    rel_row = tile_of_slot // col_tiles - here + 1
    pick = rel_row * col_tiles + tile_of_slot % col_tiles
    select = (pick[:, None] == jnp.arange(3 * col_tiles, dtype=jnp.int32)[None, :]).astype(
        jnp.bfloat16
    )
    outgoing = jnp.einsum(
        "ms,sab->mab", select, parts.reshape(3 * col_tiles, 2, -1), preferred_element_type=jnp.float32
    ).astype(jnp.bfloat16)
    incoming = lax.all_to_all(outgoing, ("grp", "tile"), 0, 0, tiled=True)
    total = jnp.sum(
        incoming.astype(jnp.float32).reshape(slots, 1, comps, ctrl_rows * ctrl_cols), axis=0
    )
    return total


def solution(mesh):
    placed = (P("grp", "tile", None, None), P("grp"), P(), P(), P(), P(), P())
    return jax.shard_map(
        local, mesh=mesh, in_specs=placed, out_specs=P(("grp", "tile"), None, None), check_vma=False
    )
```

```python
import functools

import jax
import jax.numpy as jnp
from jax import lax
from jax.experimental import pallas as pl
from jax.experimental.pallas import tpu as pltpu
from jax.sharding import PartitionSpec as P


def fold_kernel(w_ref, taps_ref, cols_ref, rows_ref, sens_ref, out_ref, ct_ref, taps_row):
    insts, comps, rows, cols = sens_ref.shape
    ctrl, tile = cols_ref.shape
    col_tiles = cols // tile
    period = taps_row.shape[1]
    half = (taps_ref.shape[0] - 1) // 2

    taps_row[...] = jnp.zeros(taps_row.shape, jnp.float32)
    taps_row[:, : taps_ref.shape[0]] = taps_ref[...].astype(jnp.float32)[None, :]
    base = jnp.broadcast_to(taps_row[...], (tile, period))
    blocks = []
    for b in range(3):
        rolled = pltpu.roll(base, (-(tile * (b - 1) + half)) % period, 1, stride=1, stride_axis=0)
        blocks.append(rolled[:, :tile])
    toeplitz = jnp.concatenate(blocks, axis=1).astype(jnp.bfloat16)
    bases = jnp.concatenate([cols_ref[...], rows_ref[...]], axis=0)
    smoothed = jnp.dot(bases, toeplitz, preferred_element_type=jnp.float32)

    ct_ref[...] = jnp.zeros(ct_ref.shape, jnp.float32)
    for y in range(col_tiles):
        for cb in range(max(0, y - 1), min(col_tiles, y + 2)):
            b = cb - y + 1
            ct_ref[ctrl * y : ctrl * (y + 1), tile * cb : tile * (cb + 1)] = smoothed[
                :ctrl, tile * b : tile * (b + 1)
            ]
    ct = ct_ref[...].astype(jnp.bfloat16)
    rows_matrix = jnp.concatenate(
        [smoothed[ctrl:, tile * (2 - d) : tile * (3 - d)] for d in range(3)], axis=0
    )
    nt = (((1,), (1,)), ((), ()))
    for k in range(comps):
        summed = (sens_ref[0, k].astype(jnp.float32) * w_ref[0]).astype(jnp.float32)
        for i in range(1, insts):
            summed = summed + sens_ref[i, k].astype(jnp.float32) * w_ref[i]
        summed = summed.astype(jnp.bfloat16)
        by_cols = lax.dot_general(summed, ct, nt, preferred_element_type=jnp.float32)
        out_ref[k] = jnp.dot(
            rows_matrix, by_cols, precision=lax.Precision.HIGHEST, preferred_element_type=jnp.float32
        ).astype(out_ref.dtype)


def local(sensitivity, inst_weight, filter_taps, basis_rows, basis_cols, box_table, owner_perm):
    tile_rows, ctrl_rows = basis_rows.shape
    tile_cols, ctrl_cols = basis_cols.shape
    insts, local_rows, comps, cols_all = sensitivity.shape
    col_tiles = cols_all // tile_cols
    slots = owner_perm.shape[0]
    assert local_rows == tile_rows and tile_rows == tile_cols and ctrl_rows == ctrl_cols

    period = 4 * tile_rows
    parts = pl.pallas_call(
        fold_kernel,
        out_shape=jax.ShapeDtypeStruct((comps, 3 * ctrl_rows, col_tiles * ctrl_cols), jnp.bfloat16),
        in_specs=[pl.BlockSpec(memory_space=pltpu.SMEM)] + [pl.BlockSpec(memory_space=pltpu.VMEM)] * 4,
        out_specs=pl.BlockSpec(memory_space=pltpu.VMEM),
        scratch_shapes=[
            pltpu.VMEM((col_tiles * ctrl_cols, cols_all), jnp.float32),
            pltpu.VMEM((1, period), jnp.float32),
        ],
    )(
        inst_weight,
        filter_taps,
        basis_cols.T,
        basis_rows.T,
        jnp.transpose(sensitivity, (0, 2, 1, 3)),
    )
    parts = parts.reshape(comps, 3, ctrl_rows, col_tiles, ctrl_cols)
    parts = parts.transpose(1, 3, 0, 2, 4).reshape(3 * col_tiles, comps * ctrl_rows * ctrl_cols)

    tiles = jnp.arange(box_table.shape[0], dtype=jnp.int32)
    tile_of_slot = jnp.sum(
        jnp.where(box_table[:, 0][None, :] == owner_perm[:, None], tiles[None, :], 0), axis=1
    )
    here = lax.axis_index("tile")
    rel_row = tile_of_slot // col_tiles - here + 1
    pick = rel_row * col_tiles + tile_of_slot % col_tiles
    select = (pick[:, None] == jnp.arange(3 * col_tiles, dtype=jnp.int32)[None, :]).astype(
        jnp.bfloat16
    )
    outgoing = jnp.einsum(
        "ms,sab->mab", select, parts.reshape(3 * col_tiles, 2, -1), preferred_element_type=jnp.float32
    ).astype(jnp.bfloat16)
    incoming = lax.all_to_all(outgoing, ("grp", "tile"), 0, 0, tiled=True)
    total = jnp.sum(
        incoming.astype(jnp.float32).reshape(slots, 1, comps, ctrl_rows * ctrl_cols), axis=0
    )
    return total


def solution(mesh):
    placed = (P("grp", "tile", None, None), P("grp"), P(), P(), P(), P(), P())
    return jax.shard_map(
        local, mesh=mesh, in_specs=placed, out_specs=P(("grp", "tile"), None, None), check_vma=False
    )
```

```python
import functools

import jax
import jax.numpy as jnp
from jax import lax
from jax.experimental import pallas as pl
from jax.experimental.pallas import tpu as pltpu
from jax.sharding import PartitionSpec as P


def fold_kernel(w_ref, taps_ref, cols_ref, rows_ref, sens_ref, out_ref, ct_ref, taps_row):
    insts, comps, rows, cols = sens_ref.shape
    ctrl, tile = cols_ref.shape
    col_tiles = cols // tile
    period = taps_row.shape[1]
    half = (taps_ref.shape[0] - 1) // 2

    taps_row[...] = jnp.zeros(taps_row.shape, jnp.float32)
    taps_row[:, : taps_ref.shape[0]] = taps_ref[...].astype(jnp.float32)[None, :]
    base = jnp.broadcast_to(taps_row[...], (tile, period))
    blocks = []
    for b in range(3):
        rolled = pltpu.roll(base, (-(tile * (b - 1) + half)) % period, 1, stride=1, stride_axis=0)
        blocks.append(rolled[:, :tile])
    toeplitz = jnp.concatenate(blocks, axis=1).astype(jnp.bfloat16)
    bases = jnp.concatenate([cols_ref[...], rows_ref[...]], axis=0)
    smoothed = jnp.dot(bases, toeplitz, preferred_element_type=jnp.float32)

    ct_ref[...] = jnp.zeros(ct_ref.shape, jnp.float32)
    for y in range(col_tiles):
        for cb in range(max(0, y - 1), min(col_tiles, y + 2)):
            b = cb - y + 1
            ct_ref[ctrl * y : ctrl * (y + 1), tile * cb : tile * (cb + 1)] = smoothed[
                :ctrl, tile * b : tile * (b + 1)
            ]
    ct = ct_ref[...]
    ct_hi = ct.astype(jnp.bfloat16)
    ct_lo = (ct - ct_hi.astype(jnp.float32)).astype(jnp.bfloat16)
    rows_matrix = jnp.concatenate(
        [smoothed[ctrl:, tile * (2 - d) : tile * (3 - d)] for d in range(3)], axis=0
    )
    nt = (((1,), (1,)), ((), ()))
    for k in range(comps):
        by_cols = None
        for i in range(insts):
            lines = sens_ref[i, k]
            term = lax.dot_general(lines, ct_hi, nt, preferred_element_type=jnp.float32)
            term = term + lax.dot_general(lines, ct_lo, nt, preferred_element_type=jnp.float32)
            term = term * w_ref[i]
            by_cols = term if by_cols is None else by_cols + term
        out_ref[k] = jnp.dot(
            rows_matrix, by_cols, precision=lax.Precision.HIGHEST, preferred_element_type=jnp.float32
        ).astype(out_ref.dtype)


def local(sensitivity, inst_weight, filter_taps, basis_rows, basis_cols, box_table, owner_perm):
    tile_rows, ctrl_rows = basis_rows.shape
    tile_cols, ctrl_cols = basis_cols.shape
    insts, local_rows, comps, cols_all = sensitivity.shape
    col_tiles = cols_all // tile_cols
    slots = owner_perm.shape[0]
    assert local_rows == tile_rows and tile_rows == tile_cols and ctrl_rows == ctrl_cols

    period = 4 * tile_rows
    parts = pl.pallas_call(
        fold_kernel,
        out_shape=jax.ShapeDtypeStruct((comps, 3 * ctrl_rows, col_tiles * ctrl_cols), jnp.bfloat16),
        in_specs=[pl.BlockSpec(memory_space=pltpu.SMEM)] + [pl.BlockSpec(memory_space=pltpu.VMEM)] * 4,
        out_specs=pl.BlockSpec(memory_space=pltpu.VMEM),
        scratch_shapes=[
            pltpu.VMEM((col_tiles * ctrl_cols, cols_all), jnp.float32),
            pltpu.VMEM((1, period), jnp.float32),
        ],
    )(
        inst_weight,
        filter_taps,
        basis_cols.T,
        basis_rows.T,
        jnp.transpose(sensitivity, (0, 2, 1, 3)),
    )
    parts = parts.reshape(comps, 3, ctrl_rows, col_tiles, ctrl_cols)
    parts = parts.transpose(1, 3, 0, 2, 4).reshape(3 * col_tiles, comps * ctrl_rows * ctrl_cols)

    tiles = jnp.arange(box_table.shape[0], dtype=jnp.int32)
    tile_of_slot = jnp.sum(
        jnp.where(box_table[:, 0][None, :] == owner_perm[:, None], tiles[None, :], 0), axis=1
    )
    here = lax.axis_index("tile")
    rel_row = tile_of_slot // col_tiles - here + 1
    pick = rel_row * col_tiles + tile_of_slot % col_tiles
    select = (pick[:, None] == jnp.arange(3 * col_tiles, dtype=jnp.int32)[None, :]).astype(
        jnp.bfloat16
    )
    outgoing = jnp.einsum(
        "ms,sab->mab", select, parts.reshape(3 * col_tiles, 2, -1), preferred_element_type=jnp.float32
    ).astype(jnp.bfloat16)
    incoming = lax.all_to_all(outgoing, ("grp", "tile"), 0, 0, tiled=True)
    total = jnp.sum(
        incoming.astype(jnp.float32).reshape(slots, 1, comps, ctrl_rows * ctrl_cols), axis=0
    )
    return total


def solution(mesh):
    placed = (P("grp", "tile", None, None), P("grp"), P(), P(), P(), P(), P())
    return jax.shard_map(
        local, mesh=mesh, in_specs=placed, out_specs=P(("grp", "tile"), None, None), check_vma=False
    )
```

```python
import functools

import jax
import jax.numpy as jnp
from jax import lax
from jax.experimental import pallas as pl
from jax.experimental.pallas import tpu as pltpu
from jax.sharding import PartitionSpec as P


def fold_kernel(
    w_ref, taps_ref, cols_ref, rows_ref, sens_ref, pick_ref, out_ref, ct_ref, taps_row, parts_ref
):
    insts, comps, rows, cols = sens_ref.shape
    ctrl, tile = cols_ref.shape
    col_tiles = cols // tile
    period = taps_row.shape[1]
    half = (taps_ref.shape[0] - 1) // 2

    taps_row[...] = jnp.zeros(taps_row.shape, jnp.float32)
    taps_row[:, : taps_ref.shape[0]] = taps_ref[...].astype(jnp.float32)[None, :]
    base = jnp.broadcast_to(taps_row[...], (tile, period))
    blocks = []
    for b in range(3):
        rolled = pltpu.roll(base, (-(tile * (b - 1) + half)) % period, 1, stride=1, stride_axis=0)
        blocks.append(rolled[:, :tile])
    toeplitz = jnp.concatenate(blocks, axis=1).astype(jnp.bfloat16)
    bases = jnp.concatenate([cols_ref[...], rows_ref[...]], axis=0)
    smoothed = jnp.dot(bases, toeplitz, preferred_element_type=jnp.float32)

    ct_ref[...] = jnp.zeros(ct_ref.shape, jnp.float32)
    for y in range(col_tiles):
        for cb in range(max(0, y - 1), min(col_tiles, y + 2)):
            b = cb - y + 1
            ct_ref[ctrl * y : ctrl * (y + 1), tile * cb : tile * (cb + 1)] = smoothed[
                :ctrl, tile * b : tile * (b + 1)
            ]
    ct = ct_ref[...]
    ct_hi = ct.astype(jnp.bfloat16)
    ct_lo = (ct - ct_hi.astype(jnp.float32)).astype(jnp.bfloat16)
    rows_matrix = jnp.concatenate(
        [smoothed[ctrl:, tile * (2 - d) : tile * (3 - d)] for d in range(3)], axis=0
    )
    nt = (((1,), (1,)), ((), ()))
    for k in range(comps):
        summed = (sens_ref[0, k].astype(jnp.float32) * w_ref[0]).astype(jnp.float32)
        for i in range(1, insts):
            summed = summed + sens_ref[i, k].astype(jnp.float32) * w_ref[i]
        summed = summed.astype(jnp.bfloat16)
        by_cols = lax.dot_general(summed, ct_hi, nt, preferred_element_type=jnp.float32)
        by_cols = by_cols + lax.dot_general(summed, ct_lo, nt, preferred_element_type=jnp.float32)
        z = jnp.dot(
            rows_matrix, by_cols, precision=lax.Precision.HIGHEST, preferred_element_type=jnp.float32
        ).astype(jnp.bfloat16)
        block = ctrl * ctrl
        parts_ref[:, block * k : block * (k + 1)] = pltpu.einshape(
            "(dp)(yq)->(dy)(pq)", z, d=3, p=ctrl, y=col_tiles, q=ctrl
        )
    select = (
        pick_ref[...] == lax.broadcasted_iota(jnp.int32, (out_ref.shape[0], parts_ref.shape[0]), 1)
    ).astype(jnp.bfloat16)
    chosen = jnp.dot(select, parts_ref[...], preferred_element_type=jnp.float32).astype(
        out_ref.dtype
    )
    half_row = out_ref.shape[2]
    out_ref[:, 0, :] = chosen[:, :half_row]
    out_ref[:, 1, :] = chosen[:, half_row:]


def local(sensitivity, inst_weight, filter_taps, basis_rows, basis_cols, box_table, owner_perm):
    tile_rows, ctrl_rows = basis_rows.shape
    tile_cols, ctrl_cols = basis_cols.shape
    insts, local_rows, comps, cols_all = sensitivity.shape
    col_tiles = cols_all // tile_cols
    slots = owner_perm.shape[0]
    assert local_rows == tile_rows and tile_rows == tile_cols and ctrl_rows == ctrl_cols

    period = 4 * tile_rows
    tiles = jnp.arange(box_table.shape[0], dtype=jnp.int32)
    tile_of_slot = jnp.sum(
        jnp.where(box_table[:, 0][None, :] == owner_perm[:, None], tiles[None, :], 0),
        axis=1,
        keepdims=True,
    )
    here = lax.axis_index("tile")
    rel_row = tile_of_slot // col_tiles - here + 1
    pick = rel_row * col_tiles + tile_of_slot % col_tiles
    values = comps * ctrl_rows * ctrl_cols
    outgoing = pl.pallas_call(
        fold_kernel,
        out_shape=jax.ShapeDtypeStruct((slots, 2, values // 2), jnp.bfloat16),
        in_specs=[pl.BlockSpec(memory_space=pltpu.SMEM)] + [pl.BlockSpec(memory_space=pltpu.VMEM)] * 5,
        out_specs=pl.BlockSpec(memory_space=pltpu.VMEM),
        scratch_shapes=[
            pltpu.VMEM((col_tiles * ctrl_cols, cols_all), jnp.float32),
            pltpu.VMEM((1, period), jnp.float32),
            pltpu.VMEM((3 * col_tiles, values), jnp.bfloat16),
        ],
    )(
        inst_weight,
        filter_taps,
        basis_cols.T,
        basis_rows.T,
        jnp.transpose(sensitivity, (0, 2, 1, 3)),
        pick,
    )
    incoming = lax.all_to_all(outgoing, ("grp", "tile"), 0, 0, tiled=True)
    total = jnp.sum(
        incoming.astype(jnp.float32).reshape(slots, 1, comps, ctrl_rows * ctrl_cols), axis=0
    )
    return total


def solution(mesh):
    placed = (P("grp", "tile", None, None), P("grp"), P(), P(), P(), P(), P())
    mapped = jax.shard_map(
        local, mesh=mesh, in_specs=placed, out_specs=P(("grp", "tile"), None, None), check_vma=False
    )

    def run(*args):
        with jax.sharding.use_abstract_mesh(mesh.abstract_mesh):
            return mapped(*args)

    return run
```

```python
import functools

import jax
import jax.numpy as jnp
from jax import lax
from jax.experimental import pallas as pl
from jax.experimental.pallas import tpu as pltpu
from jax.sharding import PartitionSpec as P


def fold_kernel(
    w_ref, taps_ref, cols_ref, rows_ref, sens_ref, box_ref, owner_ref, out_ref, ct_ref, taps_row, parts_ref
):
    insts, comps, rows, cols = sens_ref.shape
    ctrl, tile = cols_ref.shape
    col_tiles = cols // tile
    period = taps_row.shape[1]
    half = (taps_ref.shape[0] - 1) // 2

    taps_row[...] = jnp.zeros(taps_row.shape, jnp.float32)
    taps_row[:, : taps_ref.shape[0]] = taps_ref[...].astype(jnp.float32)[None, :]
    base = jnp.broadcast_to(taps_row[...], (tile, period))
    blocks = []
    for b in range(3):
        rolled = pltpu.roll(base, (-(tile * (b - 1) + half)) % period, 1, stride=1, stride_axis=0)
        blocks.append(rolled[:, :tile])
    toeplitz = jnp.concatenate(blocks, axis=1).astype(jnp.bfloat16)
    bases = jnp.concatenate([cols_ref[...], rows_ref[...]], axis=0)
    smoothed = jnp.dot(bases, toeplitz, preferred_element_type=jnp.float32)

    ct_ref[...] = jnp.zeros(ct_ref.shape, jnp.float32)
    for y in range(col_tiles):
        for cb in range(max(0, y - 1), min(col_tiles, y + 2)):
            b = cb - y + 1
            ct_ref[ctrl * y : ctrl * (y + 1), tile * cb : tile * (cb + 1)] = smoothed[
                :ctrl, tile * b : tile * (b + 1)
            ]
    ct = ct_ref[...]
    ct_hi = ct.astype(jnp.bfloat16)
    ct_lo = (ct - ct_hi.astype(jnp.float32)).astype(jnp.bfloat16)
    rows_matrix = jnp.concatenate(
        [smoothed[ctrl:, tile * (2 - d) : tile * (3 - d)] for d in range(3)], axis=0
    )
    nt = (((1,), (1,)), ((), ()))
    for k in range(comps):
        summed = (sens_ref[0, k].astype(jnp.float32) * w_ref[0]).astype(jnp.float32)
        for i in range(1, insts):
            summed = summed + sens_ref[i, k].astype(jnp.float32) * w_ref[i]
        summed = summed.astype(jnp.bfloat16)
        by_cols = lax.dot_general(summed, ct_hi, nt, preferred_element_type=jnp.float32)
        by_cols = by_cols + lax.dot_general(summed, ct_lo, nt, preferred_element_type=jnp.float32)
        z = jnp.dot(
            rows_matrix, by_cols, precision=lax.Precision.HIGHEST, preferred_element_type=jnp.float32
        ).astype(jnp.bfloat16)
        block = ctrl * ctrl
        parts_ref[:, block * k : block * (k + 1)] = pltpu.einshape(
            "(dp)(yq)->(dy)(pq)", z, d=3, p=ctrl, y=col_tiles, q=ctrl
        )
    slots = owner_ref.shape[0]
    ntiles = box_ref.shape[0]
    owner_col = jnp.broadcast_to(owner_ref[...][None, :], (8, slots)).T[:, :1]
    slot_tile = (owner_col == box_ref[...][None, :]).astype(jnp.bfloat16)
    here = lax.axis_index("tile")
    rows_of_parts = parts_ref.shape[0]
    tile_part = (
        lax.broadcasted_iota(jnp.int32, (ntiles, rows_of_parts), 0)
        == lax.broadcasted_iota(jnp.int32, (ntiles, rows_of_parts), 1) + col_tiles * (here - 1)
    ).astype(jnp.bfloat16)
    select = jnp.dot(slot_tile, tile_part, preferred_element_type=jnp.float32).astype(jnp.bfloat16)
    chosen = jnp.dot(select, parts_ref[...], preferred_element_type=jnp.float32).astype(
        out_ref.dtype
    )
    half_row = out_ref.shape[2]
    out_ref[:, 0, :] = chosen[:, :half_row]
    out_ref[:, 1, :] = chosen[:, half_row:]


def local(sensitivity, inst_weight, filter_taps, basis_rows, basis_cols, box_table, owner_perm):
    tile_rows, ctrl_rows = basis_rows.shape
    tile_cols, ctrl_cols = basis_cols.shape
    insts, local_rows, comps, cols_all = sensitivity.shape
    col_tiles = cols_all // tile_cols
    slots = owner_perm.shape[0]
    assert local_rows == tile_rows and tile_rows == tile_cols and ctrl_rows == ctrl_cols

    period = 4 * tile_rows
    values = comps * ctrl_rows * ctrl_cols
    outgoing = pl.pallas_call(
        fold_kernel,
        out_shape=jax.ShapeDtypeStruct((slots, 2, values // 2), jnp.bfloat16),
        in_specs=[pl.BlockSpec(memory_space=pltpu.SMEM)] + [pl.BlockSpec(memory_space=pltpu.VMEM)] * 6,
        out_specs=pl.BlockSpec(memory_space=pltpu.VMEM),
        scratch_shapes=[
            pltpu.VMEM((col_tiles * ctrl_cols, cols_all), jnp.float32),
            pltpu.VMEM((1, period), jnp.float32),
            pltpu.VMEM((3 * col_tiles, values), jnp.bfloat16),
        ],
    )(
        inst_weight,
        filter_taps,
        basis_cols.T,
        basis_rows.T,
        jnp.transpose(sensitivity, (0, 2, 1, 3)),
        box_table[:, 0],
        owner_perm,
    )
    incoming = lax.all_to_all(outgoing, ("grp", "tile"), 0, 0, tiled=True)
    total = jnp.sum(
        incoming.astype(jnp.float32).reshape(slots, 1, comps, ctrl_rows * ctrl_cols), axis=0
    )
    return total


def solution(mesh):
    placed = (P("grp", "tile", None, None), P("grp"), P(), P(), P(), P(), P())
    mapped = jax.shard_map(
        local, mesh=mesh, in_specs=placed, out_specs=P(("grp", "tile"), None, None), check_vma=False
    )

    def run(*args):
        with jax.sharding.use_abstract_mesh(mesh.abstract_mesh):
            return mapped(*args)

    return run
```

```python
import functools

import jax
import jax.numpy as jnp
from jax import lax
from jax.experimental import pallas as pl
from jax.experimental.pallas import tpu as pltpu
from jax.sharding import PartitionSpec as P


def fold_kernel(
    w_ref, taps_ref, cols_ref, rows_ref, sens_ref, box_ref, owner_ref, out_ref, ct_ref, taps_row, parts_ref
):
    insts, comps, rows, cols = sens_ref.shape
    ctrl, tile = cols_ref.shape
    col_tiles = cols // tile
    period = taps_row.shape[1]
    half = (taps_ref.shape[0] - 1) // 2

    taps_row[...] = jnp.zeros(taps_row.shape, jnp.float32)
    taps_row[:, : taps_ref.shape[0]] = taps_ref[...].astype(jnp.float32)[None, :]
    base = jnp.broadcast_to(taps_row[...], (tile, period))
    blocks = []
    for b in range(3):
        rolled = pltpu.roll(base, (-(tile * (b - 1) + half)) % period, 1, stride=1, stride_axis=0)
        blocks.append(rolled[:, :tile])
    toeplitz = jnp.concatenate(blocks, axis=1).astype(jnp.bfloat16)
    bases = jnp.concatenate([cols_ref[...], rows_ref[...]], axis=0)
    smoothed = jnp.dot(bases, toeplitz, preferred_element_type=jnp.float32)

    ct_ref[...] = jnp.zeros(ct_ref.shape, jnp.float32)
    for y in range(col_tiles):
        for cb in range(max(0, y - 1), min(col_tiles, y + 2)):
            b = cb - y + 1
            ct_ref[ctrl * y : ctrl * (y + 1), tile * cb : tile * (cb + 1)] = smoothed[
                :ctrl, tile * b : tile * (b + 1)
            ]
    ct = ct_ref[...]
    ct_hi = ct.astype(jnp.bfloat16)
    ct_lo = (ct - ct_hi.astype(jnp.float32)).astype(jnp.bfloat16)
    rows_matrix = jnp.concatenate(
        [smoothed[ctrl:, tile * (2 - d) : tile * (3 - d)] for d in range(3)], axis=0
    )
    nt = (((1,), (1,)), ((), ()))
    for k in range(comps):
        summed = (sens_ref[0, k].astype(jnp.float32) * w_ref[0]).astype(jnp.float32)
        for i in range(1, insts):
            summed = summed + sens_ref[i, k].astype(jnp.float32) * w_ref[i]
        summed = summed.astype(jnp.bfloat16)
        by_cols = lax.dot_general(summed, ct_hi, nt, preferred_element_type=jnp.float32)
        by_cols = by_cols + lax.dot_general(summed, ct_lo, nt, preferred_element_type=jnp.float32)
        z = jnp.dot(
            rows_matrix, by_cols, precision=lax.Precision.HIGHEST, preferred_element_type=jnp.float32
        ).astype(jnp.bfloat16)
        block = ctrl * ctrl
        parts_ref[:, block * k : block * (k + 1)] = pltpu.einshape(
            "(dp)(yq)->(dy)(pq)", z, d=3, p=ctrl, y=col_tiles, q=ctrl
        )
    slots = owner_ref.shape[0]
    ntiles = box_ref.shape[0]
    owner_col = jnp.broadcast_to(owner_ref[...][None, :], (8, slots)).T[:, :1]
    slot_tile = (owner_col == box_ref[...][None, :]).astype(jnp.bfloat16)
    here = lax.axis_index("tile")
    rows_of_parts = parts_ref.shape[0]
    tile_part = (
        lax.broadcasted_iota(jnp.int32, (ntiles, rows_of_parts), 0)
        == lax.broadcasted_iota(jnp.int32, (ntiles, rows_of_parts), 1) + col_tiles * (here - 1)
    ).astype(jnp.bfloat16)
    select = jnp.dot(slot_tile, tile_part, preferred_element_type=jnp.float32).astype(jnp.bfloat16)
    chosen = jnp.dot(select, parts_ref[...], preferred_element_type=jnp.float32).astype(
        out_ref.dtype
    )
    half_row = out_ref.shape[2]
    out_ref[:, 0, :] = chosen[:, :half_row]
    out_ref[:, 1, :] = chosen[:, half_row:]


def sum_kernel(in_ref, out_ref):
    out_ref[...] = jnp.sum(in_ref[...].astype(jnp.float32), axis=0)


def local(sensitivity, inst_weight, filter_taps, basis_rows, basis_cols, box_table, owner_perm):
    tile_rows, ctrl_rows = basis_rows.shape
    tile_cols, ctrl_cols = basis_cols.shape
    insts, local_rows, comps, cols_all = sensitivity.shape
    col_tiles = cols_all // tile_cols
    slots = owner_perm.shape[0]
    assert local_rows == tile_rows and tile_rows == tile_cols and ctrl_rows == ctrl_cols

    period = 4 * tile_rows
    values = comps * ctrl_rows * ctrl_cols
    outgoing = pl.pallas_call(
        fold_kernel,
        out_shape=jax.ShapeDtypeStruct((slots, 2, values // 2), jnp.bfloat16),
        in_specs=[pl.BlockSpec(memory_space=pltpu.SMEM)] + [pl.BlockSpec(memory_space=pltpu.VMEM)] * 6,
        out_specs=pl.BlockSpec(memory_space=pltpu.VMEM),
        scratch_shapes=[
            pltpu.VMEM((col_tiles * ctrl_cols, cols_all), jnp.float32),
            pltpu.VMEM((1, period), jnp.float32),
            pltpu.VMEM((3 * col_tiles, values), jnp.bfloat16),
        ],
    )(
        inst_weight,
        filter_taps,
        basis_cols.T,
        basis_rows.T,
        jnp.transpose(sensitivity, (0, 2, 1, 3)),
        box_table[:, 0],
        owner_perm,
    )
    incoming = lax.all_to_all(outgoing, ("grp", "tile"), 0, 0, tiled=True)
    total = pl.pallas_call(
        sum_kernel,
        out_shape=jax.ShapeDtypeStruct(incoming.shape[1:], jnp.float32),
        in_specs=[pl.BlockSpec(memory_space=pltpu.VMEM)],
        out_specs=pl.BlockSpec(memory_space=pltpu.VMEM),
    )(incoming)
    return total.reshape(1, comps, ctrl_rows * ctrl_cols)


def solution(mesh):
    placed = (P("grp", "tile", None, None), P("grp"), P(), P(), P(), P(), P())
    mapped = jax.shard_map(
        local, mesh=mesh, in_specs=placed, out_specs=P(("grp", "tile"), None, None), check_vma=False
    )

    def run(*args):
        with jax.sharding.use_abstract_mesh(mesh.abstract_mesh):
            return mapped(*args)

    return run
```

```python
import functools

import jax
import jax.numpy as jnp
from jax import lax
from jax.experimental import pallas as pl
from jax.experimental.pallas import tpu as pltpu
from jax.sharding import PartitionSpec as P


def fold_kernel(
    w_ref,
    taps_ref,
    cols_ref,
    rows_ref,
    sens_hbm,
    box_ref,
    owner_ref,
    out_ref,
    ct_ref,
    taps_row,
    parts_ref,
    sens_ref,
    sems,
):
    insts, comps, rows, cols = sens_ref.shape
    copies = [
        pltpu.make_async_copy(sens_hbm.at[:, k], sens_ref.at[:, k], sems.at[k]) for k in range(comps)
    ]
    for copy in copies:
        copy.start()
    ctrl, tile = cols_ref.shape
    col_tiles = cols // tile
    period = taps_row.shape[1]
    half = (taps_ref.shape[0] - 1) // 2

    taps_row[...] = jnp.zeros(taps_row.shape, jnp.float32)
    taps_row[:, : taps_ref.shape[0]] = taps_ref[...].astype(jnp.float32)[None, :]
    base = jnp.broadcast_to(taps_row[...], (tile, period))
    blocks = []
    for b in range(3):
        rolled = pltpu.roll(base, (-(tile * (b - 1) + half)) % period, 1, stride=1, stride_axis=0)
        blocks.append(rolled[:, :tile])
    toeplitz = jnp.concatenate(blocks, axis=1).astype(jnp.bfloat16)
    bases = jnp.concatenate([cols_ref[...], rows_ref[...]], axis=0)
    smoothed = jnp.dot(bases, toeplitz, preferred_element_type=jnp.float32)

    ct_ref[...] = jnp.zeros(ct_ref.shape, jnp.float32)
    for y in range(col_tiles):
        for cb in range(max(0, y - 1), min(col_tiles, y + 2)):
            b = cb - y + 1
            ct_ref[ctrl * y : ctrl * (y + 1), tile * cb : tile * (cb + 1)] = smoothed[
                :ctrl, tile * b : tile * (b + 1)
            ]
    ct = ct_ref[...]
    ct_hi = ct.astype(jnp.bfloat16)
    ct_lo = (ct - ct_hi.astype(jnp.float32)).astype(jnp.bfloat16)
    rows_matrix = jnp.concatenate(
        [smoothed[ctrl:, tile * (2 - d) : tile * (3 - d)] for d in range(3)], axis=0
    )
    nt = (((1,), (1,)), ((), ()))
    for k in range(comps):
        copies[k].wait()
        summed = (sens_ref[0, k].astype(jnp.float32) * w_ref[0]).astype(jnp.float32)
        for i in range(1, insts):
            summed = summed + sens_ref[i, k].astype(jnp.float32) * w_ref[i]
        summed = summed.astype(jnp.bfloat16)
        by_cols = lax.dot_general(summed, ct_hi, nt, preferred_element_type=jnp.float32)
        by_cols = by_cols + lax.dot_general(summed, ct_lo, nt, preferred_element_type=jnp.float32)
        z = jnp.dot(
            rows_matrix, by_cols, precision=lax.Precision.HIGHEST, preferred_element_type=jnp.float32
        ).astype(jnp.bfloat16)
        block = ctrl * ctrl
        parts_ref[:, block * k : block * (k + 1)] = pltpu.einshape(
            "(dp)(yq)->(dy)(pq)", z, d=3, p=ctrl, y=col_tiles, q=ctrl
        )
    slots = owner_ref.shape[0]
    ntiles = box_ref.shape[0]
    owner_col = jnp.broadcast_to(owner_ref[...][None, :], (8, slots)).T[:, :1]
    slot_tile = (owner_col == box_ref[...][None, :]).astype(jnp.bfloat16)
    here = lax.axis_index("tile")
    rows_of_parts = parts_ref.shape[0]
    tile_part = (
        lax.broadcasted_iota(jnp.int32, (ntiles, rows_of_parts), 0)
        == lax.broadcasted_iota(jnp.int32, (ntiles, rows_of_parts), 1) + col_tiles * (here - 1)
    ).astype(jnp.bfloat16)
    select = jnp.dot(slot_tile, tile_part, preferred_element_type=jnp.float32).astype(jnp.bfloat16)
    chosen = jnp.dot(select, parts_ref[...], preferred_element_type=jnp.float32).astype(
        out_ref.dtype
    )
    half_row = out_ref.shape[2]
    out_ref[:, 0, :] = chosen[:, :half_row]
    out_ref[:, 1, :] = chosen[:, half_row:]


def local(sensitivity, inst_weight, filter_taps, basis_rows, basis_cols, box_table, owner_perm):
    tile_rows, ctrl_rows = basis_rows.shape
    tile_cols, ctrl_cols = basis_cols.shape
    insts, local_rows, comps, cols_all = sensitivity.shape
    col_tiles = cols_all // tile_cols
    slots = owner_perm.shape[0]
    assert local_rows == tile_rows and tile_rows == tile_cols and ctrl_rows == ctrl_cols

    period = 4 * tile_rows
    values = comps * ctrl_rows * ctrl_cols
    outgoing = pl.pallas_call(
        fold_kernel,
        out_shape=jax.ShapeDtypeStruct((slots, 2, values // 2), jnp.bfloat16),
        in_specs=[pl.BlockSpec(memory_space=pltpu.SMEM)]
        + [pl.BlockSpec(memory_space=pltpu.VMEM)] * 3
        + [pl.BlockSpec(memory_space=pl.ANY)]
        + [pl.BlockSpec(memory_space=pltpu.VMEM)] * 2,
        out_specs=pl.BlockSpec(memory_space=pltpu.VMEM),
        scratch_shapes=[
            pltpu.VMEM((col_tiles * ctrl_cols, cols_all), jnp.float32),
            pltpu.VMEM((1, period), jnp.float32),
            pltpu.VMEM((3 * col_tiles, values), jnp.bfloat16),
            pltpu.VMEM((insts, comps, local_rows, cols_all), sensitivity.dtype),
            pltpu.SemaphoreType.DMA((comps,)),
        ],
    )(
        inst_weight,
        filter_taps,
        basis_cols.T,
        basis_rows.T,
        jnp.transpose(sensitivity, (0, 2, 1, 3)),
        box_table[:, 0],
        owner_perm,
    )
    incoming = lax.all_to_all(outgoing, ("grp", "tile"), 0, 0, tiled=True)
    total = jnp.sum(
        incoming.astype(jnp.float32).reshape(slots, 1, comps, ctrl_rows * ctrl_cols), axis=0
    )
    return total


def solution(mesh):
    placed = (P("grp", "tile", None, None), P("grp"), P(), P(), P(), P(), P())
    mapped = jax.shard_map(
        local, mesh=mesh, in_specs=placed, out_specs=P(("grp", "tile"), None, None), check_vma=False
    )

    def run(*args):
        with jax.sharding.use_abstract_mesh(mesh.abstract_mesh):
            return mapped(*args)

    return run
```

```python
import functools

import jax
import jax.numpy as jnp
from jax import lax
from jax.experimental import pallas as pl
from jax.experimental.pallas import tpu as pltpu
from jax.sharding import PartitionSpec as P


def fold_kernel(
    w_ref, taps_ref, cols_ref, rows_ref, sens_ref, box_ref, owner_ref, out_ref, ct_ref, taps_row, parts_ref
):
    insts, comps, rows, cols = sens_ref.shape
    ctrl, tile = cols_ref.shape
    col_tiles = cols // tile
    period = taps_row.shape[1]
    half = (taps_ref.shape[0] - 1) // 2

    taps_row[...] = jnp.zeros(taps_row.shape, jnp.float32)
    taps_row[:, : taps_ref.shape[0]] = taps_ref[...].astype(jnp.float32)[None, :]
    base = jnp.broadcast_to(taps_row[...], (tile, period))
    blocks = []
    for b in range(3):
        rolled = pltpu.roll(base, (-(tile * (b - 1) + half)) % period, 1, stride=1, stride_axis=0)
        blocks.append(rolled[:, :tile])
    toeplitz = jnp.concatenate(blocks, axis=1).astype(jnp.bfloat16)
    bases = jnp.concatenate([cols_ref[...], rows_ref[...]], axis=0)
    smoothed = jnp.dot(bases, toeplitz, preferred_element_type=jnp.float32)

    ct_ref[...] = jnp.zeros(ct_ref.shape, jnp.float32)
    for y in range(col_tiles):
        for cb in range(max(0, y - 1), min(col_tiles, y + 2)):
            b = cb - y + 1
            ct_ref[ctrl * y : ctrl * (y + 1), tile * cb : tile * (cb + 1)] = smoothed[
                :ctrl, tile * b : tile * (b + 1)
            ]
    ct = ct_ref[...]
    ct_hi = ct.astype(jnp.bfloat16)
    ct_lo = (ct - ct_hi.astype(jnp.float32)).astype(jnp.bfloat16)
    rows_matrix = jnp.concatenate(
        [smoothed[ctrl:, tile * (2 - d) : tile * (3 - d)] for d in range(3)], axis=0
    )
    rows_hi = rows_matrix.astype(jnp.bfloat16)
    rows_lo = (rows_matrix - rows_hi.astype(jnp.float32)).astype(jnp.bfloat16)
    nt = (((1,), (1,)), ((), ()))
    for k in range(comps):
        summed = (sens_ref[0, k].astype(jnp.float32) * w_ref[0]).astype(jnp.float32)
        for i in range(1, insts):
            summed = summed + sens_ref[i, k].astype(jnp.float32) * w_ref[i]
        summed = summed.astype(jnp.bfloat16)
        by_cols = lax.dot_general(summed, ct_hi, nt, preferred_element_type=jnp.float32)
        by_cols = by_cols + lax.dot_general(summed, ct_lo, nt, preferred_element_type=jnp.float32)
        cols_hi = by_cols.astype(jnp.bfloat16)
        cols_lo = (by_cols - cols_hi.astype(jnp.float32)).astype(jnp.bfloat16)
        z = jnp.dot(rows_hi, cols_hi, preferred_element_type=jnp.float32)
        z = z + jnp.dot(rows_hi, cols_lo, preferred_element_type=jnp.float32)
        z = (z + jnp.dot(rows_lo, cols_hi, preferred_element_type=jnp.float32)).astype(jnp.bfloat16)
        block = ctrl * ctrl
        parts_ref[:, block * k : block * (k + 1)] = pltpu.einshape(
            "(dp)(yq)->(dy)(pq)", z, d=3, p=ctrl, y=col_tiles, q=ctrl
        )
    slots = owner_ref.shape[0]
    ntiles = box_ref.shape[0]
    owner_col = jnp.broadcast_to(owner_ref[...][None, :], (8, slots)).T[:, :1]
    slot_tile = (owner_col == box_ref[...][None, :]).astype(jnp.bfloat16)
    here = lax.axis_index("tile")
    rows_of_parts = parts_ref.shape[0]
    tile_part = (
        lax.broadcasted_iota(jnp.int32, (ntiles, rows_of_parts), 0)
        == lax.broadcasted_iota(jnp.int32, (ntiles, rows_of_parts), 1) + col_tiles * (here - 1)
    ).astype(jnp.bfloat16)
    select = jnp.dot(slot_tile, tile_part, preferred_element_type=jnp.float32).astype(jnp.bfloat16)
    chosen = jnp.dot(select, parts_ref[...], preferred_element_type=jnp.float32).astype(
        out_ref.dtype
    )
    half_row = out_ref.shape[2]
    out_ref[:, 0, :] = chosen[:, :half_row]
    out_ref[:, 1, :] = chosen[:, half_row:]


def local(sensitivity, inst_weight, filter_taps, basis_rows, basis_cols, box_table, owner_perm):
    tile_rows, ctrl_rows = basis_rows.shape
    tile_cols, ctrl_cols = basis_cols.shape
    insts, local_rows, comps, cols_all = sensitivity.shape
    col_tiles = cols_all // tile_cols
    slots = owner_perm.shape[0]
    assert local_rows == tile_rows and tile_rows == tile_cols and ctrl_rows == ctrl_cols

    period = 4 * tile_rows
    values = comps * ctrl_rows * ctrl_cols
    outgoing = pl.pallas_call(
        fold_kernel,
        out_shape=jax.ShapeDtypeStruct((slots, 2, values // 2), jnp.bfloat16),
        in_specs=[pl.BlockSpec(memory_space=pltpu.SMEM)] + [pl.BlockSpec(memory_space=pltpu.VMEM)] * 6,
        out_specs=pl.BlockSpec(memory_space=pltpu.VMEM),
        scratch_shapes=[
            pltpu.VMEM((col_tiles * ctrl_cols, cols_all), jnp.float32),
            pltpu.VMEM((1, period), jnp.float32),
            pltpu.VMEM((3 * col_tiles, values), jnp.bfloat16),
        ],
    )(
        inst_weight,
        filter_taps,
        basis_cols.T,
        basis_rows.T,
        jnp.transpose(sensitivity, (0, 2, 1, 3)),
        box_table[:, 0],
        owner_perm,
    )
    incoming = lax.all_to_all(outgoing, ("grp", "tile"), 0, 0, tiled=True)
    total = jnp.sum(
        incoming.astype(jnp.float32).reshape(slots, 1, comps, ctrl_rows * ctrl_cols), axis=0
    )
    return total


def solution(mesh):
    placed = (P("grp", "tile", None, None), P("grp"), P(), P(), P(), P(), P())
    mapped = jax.shard_map(
        local, mesh=mesh, in_specs=placed, out_specs=P(("grp", "tile"), None, None), check_vma=False
    )

    def run(*args):
        with jax.sharding.use_abstract_mesh(mesh.abstract_mesh):
            return mapped(*args)

    return run
```

```python
import functools

import jax
import jax.numpy as jnp
from jax import lax
from jax.experimental import pallas as pl
from jax.experimental.pallas import tpu as pltpu
from jax.sharding import PartitionSpec as P


def fold_kernel(
    w_ref,
    taps_ref,
    cols_ref,
    rows_ref,
    sens_hbm,
    box_ref,
    owner_ref,
    out_ref,
    ct_ref,
    taps_row,
    parts_ref,
    sens_ref,
    sem,
):
    insts, comps, rows, cols = sens_ref.shape
    arrival = pltpu.make_async_copy(sens_hbm, sens_ref, sem)
    arrival.start()
    ctrl, tile = cols_ref.shape
    col_tiles = cols // tile
    period = taps_row.shape[1]
    half = (taps_ref.shape[0] - 1) // 2

    taps_row[...] = jnp.zeros(taps_row.shape, jnp.float32)
    taps_row[:, : taps_ref.shape[0]] = taps_ref[...].astype(jnp.float32)[None, :]
    base = jnp.broadcast_to(taps_row[...], (tile, period))
    blocks = []
    for b in range(3):
        rolled = pltpu.roll(base, (-(tile * (b - 1) + half)) % period, 1, stride=1, stride_axis=0)
        blocks.append(rolled[:, :tile])
    toeplitz = jnp.concatenate(blocks, axis=1).astype(jnp.bfloat16)
    bases = jnp.concatenate([cols_ref[...], rows_ref[...]], axis=0)
    smoothed = jnp.dot(bases, toeplitz, preferred_element_type=jnp.float32)

    ct_ref[...] = jnp.zeros(ct_ref.shape, jnp.float32)
    for y in range(col_tiles):
        for cb in range(max(0, y - 1), min(col_tiles, y + 2)):
            b = cb - y + 1
            ct_ref[ctrl * y : ctrl * (y + 1), tile * cb : tile * (cb + 1)] = smoothed[
                :ctrl, tile * b : tile * (b + 1)
            ]
    ct = ct_ref[...]
    ct_hi = ct.astype(jnp.bfloat16)
    ct_lo = (ct - ct_hi.astype(jnp.float32)).astype(jnp.bfloat16)
    rows_matrix = jnp.concatenate(
        [smoothed[ctrl:, tile * (2 - d) : tile * (3 - d)] for d in range(3)], axis=0
    )
    rows_hi = rows_matrix.astype(jnp.bfloat16)
    rows_lo = (rows_matrix - rows_hi.astype(jnp.float32)).astype(jnp.bfloat16)
    nt = (((1,), (1,)), ((), ()))
    arrival.wait()
    for k in range(comps):
        summed = (sens_ref[0, k].astype(jnp.float32) * w_ref[0]).astype(jnp.float32)
        for i in range(1, insts):
            summed = summed + sens_ref[i, k].astype(jnp.float32) * w_ref[i]
        summed = summed.astype(jnp.bfloat16)
        by_cols = lax.dot_general(summed, ct_hi, nt, preferred_element_type=jnp.float32)
        by_cols = by_cols + lax.dot_general(summed, ct_lo, nt, preferred_element_type=jnp.float32)
        cols_hi = by_cols.astype(jnp.bfloat16)
        cols_lo = (by_cols - cols_hi.astype(jnp.float32)).astype(jnp.bfloat16)
        z = jnp.dot(rows_hi, cols_hi, preferred_element_type=jnp.float32)
        z = z + jnp.dot(rows_hi, cols_lo, preferred_element_type=jnp.float32)
        z = (z + jnp.dot(rows_lo, cols_hi, preferred_element_type=jnp.float32)).astype(jnp.bfloat16)
        block = ctrl * ctrl
        parts_ref[:, block * k : block * (k + 1)] = pltpu.einshape(
            "(dp)(yq)->(dy)(pq)", z, d=3, p=ctrl, y=col_tiles, q=ctrl
        )
    slots = owner_ref.shape[0]
    ntiles = box_ref.shape[0]
    owner_col = jnp.broadcast_to(owner_ref[...][None, :], (8, slots)).T[:, :1]
    slot_tile = (owner_col == box_ref[...][None, :]).astype(jnp.bfloat16)
    here = lax.axis_index("tile")
    rows_of_parts = parts_ref.shape[0]
    tile_part = (
        lax.broadcasted_iota(jnp.int32, (ntiles, rows_of_parts), 0)
        == lax.broadcasted_iota(jnp.int32, (ntiles, rows_of_parts), 1) + col_tiles * (here - 1)
    ).astype(jnp.bfloat16)
    select = jnp.dot(slot_tile, tile_part, preferred_element_type=jnp.float32).astype(jnp.bfloat16)
    chosen = jnp.dot(select, parts_ref[...], preferred_element_type=jnp.float32).astype(
        out_ref.dtype
    )
    half_row = out_ref.shape[2]
    out_ref[:, 0, :] = chosen[:, :half_row]
    out_ref[:, 1, :] = chosen[:, half_row:]


def local(sensitivity, inst_weight, filter_taps, basis_rows, basis_cols, box_table, owner_perm):
    tile_rows, ctrl_rows = basis_rows.shape
    tile_cols, ctrl_cols = basis_cols.shape
    insts, local_rows, comps, cols_all = sensitivity.shape
    col_tiles = cols_all // tile_cols
    slots = owner_perm.shape[0]
    assert local_rows == tile_rows and tile_rows == tile_cols and ctrl_rows == ctrl_cols

    period = 4 * tile_rows
    values = comps * ctrl_rows * ctrl_cols
    outgoing = pl.pallas_call(
        fold_kernel,
        out_shape=jax.ShapeDtypeStruct((slots, 2, values // 2), jnp.bfloat16),
        in_specs=[pl.BlockSpec(memory_space=pltpu.SMEM)]
        + [pl.BlockSpec(memory_space=pltpu.VMEM)] * 3
        + [pl.BlockSpec(memory_space=pl.ANY)]
        + [pl.BlockSpec(memory_space=pltpu.VMEM)] * 2,
        out_specs=pl.BlockSpec(memory_space=pltpu.VMEM),
        scratch_shapes=[
            pltpu.VMEM((col_tiles * ctrl_cols, cols_all), jnp.float32),
            pltpu.VMEM((1, period), jnp.float32),
            pltpu.VMEM((3 * col_tiles, values), jnp.bfloat16),
            pltpu.VMEM((insts, comps, local_rows, cols_all), sensitivity.dtype),
            pltpu.SemaphoreType.DMA(()),
        ],
    )(
        inst_weight,
        filter_taps,
        basis_cols.T,
        basis_rows.T,
        jnp.transpose(sensitivity, (0, 2, 1, 3)),
        box_table[:, 0],
        owner_perm,
    )
    incoming = lax.all_to_all(outgoing, ("grp", "tile"), 0, 0, tiled=True)
    total = jnp.sum(
        incoming.astype(jnp.float32).reshape(slots, 1, comps, ctrl_rows * ctrl_cols), axis=0
    )
    return total


def solution(mesh):
    placed = (P("grp", "tile", None, None), P("grp"), P(), P(), P(), P(), P())
    mapped = jax.shard_map(
        local, mesh=mesh, in_specs=placed, out_specs=P(("grp", "tile"), None, None), check_vma=False
    )

    def run(*args):
        with jax.sharding.use_abstract_mesh(mesh.abstract_mesh):
            return mapped(*args)

    return run
```

```python
import functools

import jax
import jax.numpy as jnp
from jax import lax
from jax.experimental import pallas as pl
from jax.experimental.pallas import tpu as pltpu
from jax.sharding import PartitionSpec as P


def fold_kernel(
    w_ref, taps_ref, cols_ref, rows_ref, sens_ref, box_ref, owner_ref, out_ref, taps_row, parts_ref
):
    insts, comps, rows, cols = sens_ref.shape
    ctrl, tile = cols_ref.shape
    col_tiles = cols // tile
    period = taps_row.shape[1]
    half = (taps_ref.shape[0] - 1) // 2

    taps_row[...] = jnp.zeros(taps_row.shape, jnp.float32)
    taps_row[:, : taps_ref.shape[0]] = taps_ref[...].astype(jnp.float32)[None, :]
    base = jnp.broadcast_to(taps_row[...], (tile, period))
    blocks = []
    for b in range(3):
        rolled = pltpu.roll(base, (-(tile * (b - 1) + half)) % period, 1, stride=1, stride_axis=0)
        blocks.append(rolled[:, :tile])
    toeplitz = jnp.concatenate(blocks, axis=1).astype(jnp.bfloat16)
    bases = jnp.concatenate([cols_ref[...], rows_ref[...]], axis=0)
    smoothed = jnp.dot(bases, toeplitz, preferred_element_type=jnp.float32)

    empty = jnp.zeros((ctrl, tile), jnp.float32)
    ct = jnp.concatenate(
        [
            jnp.concatenate(
                [
                    smoothed[:ctrl, tile * (cb - y + 1) : tile * (cb - y + 2)]
                    if abs(cb - y) <= 1
                    else empty
                    for cb in range(col_tiles)
                ],
                axis=1,
            )
            for y in range(col_tiles)
        ],
        axis=0,
    )
    ct_hi = ct.astype(jnp.bfloat16)
    ct_lo = (ct - ct_hi.astype(jnp.float32)).astype(jnp.bfloat16)
    rows_matrix = jnp.concatenate(
        [smoothed[ctrl:, tile * (2 - d) : tile * (3 - d)] for d in range(3)], axis=0
    )
    rows_hi = rows_matrix.astype(jnp.bfloat16)
    rows_lo = (rows_matrix - rows_hi.astype(jnp.float32)).astype(jnp.bfloat16)
    nt = (((1,), (1,)), ((), ()))
    for k in range(comps):
        summed = (sens_ref[0, k].astype(jnp.float32) * w_ref[0]).astype(jnp.float32)
        for i in range(1, insts):
            summed = summed + sens_ref[i, k].astype(jnp.float32) * w_ref[i]
        summed = summed.astype(jnp.bfloat16)
        by_cols = lax.dot_general(summed, ct_hi, nt, preferred_element_type=jnp.float32)
        by_cols = by_cols + lax.dot_general(summed, ct_lo, nt, preferred_element_type=jnp.float32)
        cols_hi = by_cols.astype(jnp.bfloat16)
        cols_lo = (by_cols - cols_hi.astype(jnp.float32)).astype(jnp.bfloat16)
        z = jnp.dot(rows_hi, cols_hi, preferred_element_type=jnp.float32)
        z = z + jnp.dot(rows_hi, cols_lo, preferred_element_type=jnp.float32)
        z = (z + jnp.dot(rows_lo, cols_hi, preferred_element_type=jnp.float32)).astype(jnp.bfloat16)
        block = ctrl * ctrl
        parts_ref[:, block * k : block * (k + 1)] = pltpu.einshape(
            "(dp)(yq)->(dy)(pq)", z, d=3, p=ctrl, y=col_tiles, q=ctrl
        )
    slots = owner_ref.shape[0]
    ntiles = box_ref.shape[0]
    owner_col = jnp.broadcast_to(owner_ref[...][None, :], (8, slots)).T[:, :1]
    slot_tile = (owner_col == box_ref[...][None, :]).astype(jnp.bfloat16)
    here = lax.axis_index("tile")
    rows_of_parts = parts_ref.shape[0]
    tile_part = (
        lax.broadcasted_iota(jnp.int32, (ntiles, rows_of_parts), 0)
        == lax.broadcasted_iota(jnp.int32, (ntiles, rows_of_parts), 1) + col_tiles * (here - 1)
    ).astype(jnp.bfloat16)
    select = jnp.dot(slot_tile, tile_part, preferred_element_type=jnp.float32).astype(jnp.bfloat16)
    chosen = jnp.dot(select, parts_ref[...], preferred_element_type=jnp.float32).astype(
        out_ref.dtype
    )
    half_row = out_ref.shape[2]
    out_ref[:, 0, :] = chosen[:, :half_row]
    out_ref[:, 1, :] = chosen[:, half_row:]


def local(sensitivity, inst_weight, filter_taps, basis_rows, basis_cols, box_table, owner_perm):
    tile_rows, ctrl_rows = basis_rows.shape
    tile_cols, ctrl_cols = basis_cols.shape
    insts, local_rows, comps, cols_all = sensitivity.shape
    col_tiles = cols_all // tile_cols
    slots = owner_perm.shape[0]
    assert local_rows == tile_rows and tile_rows == tile_cols and ctrl_rows == ctrl_cols

    period = 4 * tile_rows
    values = comps * ctrl_rows * ctrl_cols
    outgoing = pl.pallas_call(
        fold_kernel,
        out_shape=jax.ShapeDtypeStruct((slots, 2, values // 2), jnp.bfloat16),
        in_specs=[pl.BlockSpec(memory_space=pltpu.SMEM)] + [pl.BlockSpec(memory_space=pltpu.VMEM)] * 6,
        out_specs=pl.BlockSpec(memory_space=pltpu.VMEM),
        scratch_shapes=[
            pltpu.VMEM((1, period), jnp.float32),
            pltpu.VMEM((3 * col_tiles, values), jnp.bfloat16),
        ],
    )(
        inst_weight,
        filter_taps,
        basis_cols.T,
        basis_rows.T,
        jnp.transpose(sensitivity, (0, 2, 1, 3)),
        box_table[:, 0],
        owner_perm,
    )
    incoming = lax.all_to_all(outgoing, ("grp", "tile"), 0, 0, tiled=True)
    total = jnp.sum(
        incoming.astype(jnp.float32).reshape(slots, 1, comps, ctrl_rows * ctrl_cols), axis=0
    )
    return total


def solution(mesh):
    placed = (P("grp", "tile", None, None), P("grp"), P(), P(), P(), P(), P())
    mapped = jax.shard_map(
        local, mesh=mesh, in_specs=placed, out_specs=P(("grp", "tile"), None, None), check_vma=False
    )

    def run(*args):
        with jax.sharding.use_abstract_mesh(mesh.abstract_mesh):
            return mapped(*args)

    return run
```

```python
import functools

import jax
import jax.numpy as jnp
from jax import lax
from jax.experimental import pallas as pl
from jax.experimental.pallas import tpu as pltpu
from jax.sharding import PartitionSpec as P


def fold_kernel(
    w_ref, taps_ref, cols_ref, rows_ref, sens_ref, box_ref, owner_ref, out_ref, ct_ref, taps_row, parts_ref
):
    insts, comps, rows, cols = sens_ref.shape
    ctrl, tile = cols_ref.shape
    col_tiles = cols // tile
    period = taps_row.shape[1]
    half = (taps_ref.shape[0] - 1) // 2

    taps_row[...] = jnp.zeros(taps_row.shape, jnp.float32)
    taps_row[:, : taps_ref.shape[0]] = taps_ref[...].astype(jnp.float32)[None, :]
    base = jnp.broadcast_to(taps_row[...], (tile, period))
    blocks = []
    for b in range(3):
        rolled = pltpu.roll(base, (-(tile * (b - 1) + half)) % period, 1, stride=1, stride_axis=0)
        blocks.append(rolled[:, :tile])
    toeplitz = jnp.concatenate(blocks, axis=1).astype(jnp.bfloat16)
    bases = jnp.concatenate([cols_ref[...], rows_ref[...]], axis=0)
    smoothed = jnp.dot(bases, toeplitz, preferred_element_type=jnp.float32)

    ct_ref[...] = jnp.zeros(ct_ref.shape, jnp.float32)
    for y in range(col_tiles):
        for cb in range(max(0, y - 1), min(col_tiles, y + 2)):
            b = cb - y + 1
            ct_ref[ctrl * y : ctrl * (y + 1), tile * cb : tile * (cb + 1)] = smoothed[
                :ctrl, tile * b : tile * (b + 1)
            ]
    ct = ct_ref[...].astype(jnp.bfloat16)
    rows_matrix = jnp.concatenate(
        [smoothed[ctrl:, tile * (2 - d) : tile * (3 - d)] for d in range(3)], axis=0
    )
    rows_hi = rows_matrix.astype(jnp.bfloat16)
    rows_lo = (rows_matrix - rows_hi.astype(jnp.float32)).astype(jnp.bfloat16)
    nt = (((1,), (1,)), ((), ()))
    for k in range(comps):
        summed = (sens_ref[0, k].astype(jnp.float32) * w_ref[0]).astype(jnp.float32)
        for i in range(1, insts):
            summed = summed + sens_ref[i, k].astype(jnp.float32) * w_ref[i]
        summed = summed.astype(jnp.bfloat16)
        by_cols = lax.dot_general(summed, ct, nt, preferred_element_type=jnp.float32)
        cols_hi = by_cols.astype(jnp.bfloat16)
        cols_lo = (by_cols - cols_hi.astype(jnp.float32)).astype(jnp.bfloat16)
        z = jnp.dot(rows_hi, cols_hi, preferred_element_type=jnp.float32)
        z = z + jnp.dot(rows_hi, cols_lo, preferred_element_type=jnp.float32)
        z = (z + jnp.dot(rows_lo, cols_hi, preferred_element_type=jnp.float32)).astype(jnp.bfloat16)
        block = ctrl * ctrl
        parts_ref[:, block * k : block * (k + 1)] = pltpu.einshape(
            "(dp)(yq)->(dy)(pq)", z, d=3, p=ctrl, y=col_tiles, q=ctrl
        )
    slots = owner_ref.shape[0]
    ntiles = box_ref.shape[0]
    owner_col = jnp.broadcast_to(owner_ref[...][None, :], (8, slots)).T[:, :1]
    slot_tile = (owner_col == box_ref[...][None, :]).astype(jnp.bfloat16)
    here = lax.axis_index("tile")
    rows_of_parts = parts_ref.shape[0]
    tile_part = (
        lax.broadcasted_iota(jnp.int32, (ntiles, rows_of_parts), 0)
        == lax.broadcasted_iota(jnp.int32, (ntiles, rows_of_parts), 1) + col_tiles * (here - 1)
    ).astype(jnp.bfloat16)
    select = jnp.dot(slot_tile, tile_part, preferred_element_type=jnp.float32).astype(jnp.bfloat16)
    chosen = jnp.dot(select, parts_ref[...], preferred_element_type=jnp.float32).astype(
        out_ref.dtype
    )
    half_row = out_ref.shape[2]
    out_ref[:, 0, :] = chosen[:, :half_row]
    out_ref[:, 1, :] = chosen[:, half_row:]


def local(sensitivity, inst_weight, filter_taps, basis_rows, basis_cols, box_table, owner_perm):
    tile_rows, ctrl_rows = basis_rows.shape
    tile_cols, ctrl_cols = basis_cols.shape
    insts, local_rows, comps, cols_all = sensitivity.shape
    col_tiles = cols_all // tile_cols
    slots = owner_perm.shape[0]
    assert local_rows == tile_rows and tile_rows == tile_cols and ctrl_rows == ctrl_cols

    period = 4 * tile_rows
    values = comps * ctrl_rows * ctrl_cols
    outgoing = pl.pallas_call(
        fold_kernel,
        out_shape=jax.ShapeDtypeStruct((slots, 2, values // 2), jnp.bfloat16),
        in_specs=[pl.BlockSpec(memory_space=pltpu.SMEM)] + [pl.BlockSpec(memory_space=pltpu.VMEM)] * 6,
        out_specs=pl.BlockSpec(memory_space=pltpu.VMEM),
        scratch_shapes=[
            pltpu.VMEM((col_tiles * ctrl_cols, cols_all), jnp.float32),
            pltpu.VMEM((1, period), jnp.float32),
            pltpu.VMEM((3 * col_tiles, values), jnp.bfloat16),
        ],
    )(
        inst_weight,
        filter_taps,
        basis_cols.T,
        basis_rows.T,
        jnp.transpose(sensitivity, (0, 2, 1, 3)),
        box_table[:, 0],
        owner_perm,
    )
    incoming = lax.all_to_all(outgoing, ("grp", "tile"), 0, 0, tiled=True)
    total = jnp.sum(
        incoming.astype(jnp.float32).reshape(slots, 1, comps, ctrl_rows * ctrl_cols), axis=0
    )
    return total


def solution(mesh):
    placed = (P("grp", "tile", None, None), P("grp"), P(), P(), P(), P(), P())
    mapped = jax.shard_map(
        local, mesh=mesh, in_specs=placed, out_specs=P(("grp", "tile"), None, None), check_vma=False
    )

    def run(*args):
        with jax.sharding.use_abstract_mesh(mesh.abstract_mesh):
            return mapped(*args)

    return run
```

```python
import functools

import jax
import jax.numpy as jnp
from jax import lax
from jax.experimental import pallas as pl
from jax.experimental.pallas import tpu as pltpu
from jax.sharding import PartitionSpec as P


def fold_kernel(
    w_ref, taps_ref, cols_ref, rows_ref, sens_ref, box_ref, owner_ref, out_ref, ct_ref, taps_row, parts_ref
):
    insts, comps, rows, cols = sens_ref.shape
    ctrl, tile = cols_ref.shape
    col_tiles = cols // tile
    period = taps_row.shape[1]
    half = (taps_ref.shape[0] - 1) // 2

    taps_row[...] = jnp.zeros(taps_row.shape, jnp.float32)
    taps_row[:, : taps_ref.shape[0]] = taps_ref[...].astype(jnp.float32)[None, :]
    base = jnp.broadcast_to(taps_row[...], (tile, period))
    blocks = []
    for b in range(3):
        rolled = pltpu.roll(base, (-(tile * (b - 1) + half)) % period, 1, stride=1, stride_axis=0)
        blocks.append(rolled[:, :tile])
    toeplitz = jnp.concatenate(blocks, axis=1).astype(jnp.bfloat16)
    bases = jnp.concatenate([cols_ref[...], rows_ref[...]], axis=0)
    smoothed = jnp.dot(bases, toeplitz, preferred_element_type=jnp.float32)

    ct_ref[...] = jnp.zeros(ct_ref.shape, jnp.float32)
    for y in range(col_tiles):
        for cb in range(max(0, y - 1), min(col_tiles, y + 2)):
            b = cb - y + 1
            ct_ref[ctrl * y : ctrl * (y + 1), tile * cb : tile * (cb + 1)] = smoothed[
                :ctrl, tile * b : tile * (b + 1)
            ]
    ct = ct_ref[...].astype(jnp.bfloat16)
    rows_matrix = jnp.concatenate(
        [smoothed[ctrl:, tile * (2 - d) : tile * (3 - d)] for d in range(3)], axis=0
    )
    rows_hi = rows_matrix.astype(jnp.bfloat16)
    nt = (((1,), (1,)), ((), ()))
    for k in range(comps):
        summed = (sens_ref[0, k].astype(jnp.float32) * w_ref[0]).astype(jnp.float32)
        for i in range(1, insts):
            summed = summed + sens_ref[i, k].astype(jnp.float32) * w_ref[i]
        summed = summed.astype(jnp.bfloat16)
        by_cols = lax.dot_general(summed, ct, nt, preferred_element_type=jnp.float32)
        cols_hi = by_cols.astype(jnp.bfloat16)
        cols_lo = (by_cols - cols_hi.astype(jnp.float32)).astype(jnp.bfloat16)
        z = jnp.dot(rows_hi, cols_hi, preferred_element_type=jnp.float32)
        z = (z + jnp.dot(rows_hi, cols_lo, preferred_element_type=jnp.float32)).astype(jnp.bfloat16)
        block = ctrl * ctrl
        parts_ref[:, block * k : block * (k + 1)] = pltpu.einshape(
            "(dp)(yq)->(dy)(pq)", z, d=3, p=ctrl, y=col_tiles, q=ctrl
        )
    slots = owner_ref.shape[0]
    ntiles = box_ref.shape[0]
    owner_col = jnp.broadcast_to(owner_ref[...][None, :], (8, slots)).T[:, :1]
    slot_tile = (owner_col == box_ref[...][None, :]).astype(jnp.bfloat16)
    here = lax.axis_index("tile")
    rows_of_parts = parts_ref.shape[0]
    tile_part = (
        lax.broadcasted_iota(jnp.int32, (ntiles, rows_of_parts), 0)
        == lax.broadcasted_iota(jnp.int32, (ntiles, rows_of_parts), 1) + col_tiles * (here - 1)
    ).astype(jnp.bfloat16)
    select = jnp.dot(slot_tile, tile_part, preferred_element_type=jnp.float32).astype(jnp.bfloat16)
    chosen = jnp.dot(select, parts_ref[...], preferred_element_type=jnp.float32).astype(
        out_ref.dtype
    )
    half_row = out_ref.shape[2]
    out_ref[:, 0, :] = chosen[:, :half_row]
    out_ref[:, 1, :] = chosen[:, half_row:]


def local(sensitivity, inst_weight, filter_taps, basis_rows, basis_cols, box_table, owner_perm):
    tile_rows, ctrl_rows = basis_rows.shape
    tile_cols, ctrl_cols = basis_cols.shape
    insts, local_rows, comps, cols_all = sensitivity.shape
    col_tiles = cols_all // tile_cols
    slots = owner_perm.shape[0]
    assert local_rows == tile_rows and tile_rows == tile_cols and ctrl_rows == ctrl_cols

    period = 4 * tile_rows
    values = comps * ctrl_rows * ctrl_cols
    outgoing = pl.pallas_call(
        fold_kernel,
        out_shape=jax.ShapeDtypeStruct((slots, 2, values // 2), jnp.bfloat16),
        in_specs=[pl.BlockSpec(memory_space=pltpu.SMEM)] + [pl.BlockSpec(memory_space=pltpu.VMEM)] * 6,
        out_specs=pl.BlockSpec(memory_space=pltpu.VMEM),
        scratch_shapes=[
            pltpu.VMEM((col_tiles * ctrl_cols, cols_all), jnp.float32),
            pltpu.VMEM((1, period), jnp.float32),
            pltpu.VMEM((3 * col_tiles, values), jnp.bfloat16),
        ],
    )(
        inst_weight,
        filter_taps,
        basis_cols.T,
        basis_rows.T,
        jnp.transpose(sensitivity, (0, 2, 1, 3)),
        box_table[:, 0],
        owner_perm,
    )
    incoming = lax.all_to_all(outgoing, ("grp", "tile"), 0, 0, tiled=True)
    total = jnp.sum(
        incoming.astype(jnp.float32).reshape(slots, 1, comps, ctrl_rows * ctrl_cols), axis=0
    )
    return total


def solution(mesh):
    placed = (P("grp", "tile", None, None), P("grp"), P(), P(), P(), P(), P())
    mapped = jax.shard_map(
        local, mesh=mesh, in_specs=placed, out_specs=P(("grp", "tile"), None, None), check_vma=False
    )

    def run(*args):
        with jax.sharding.use_abstract_mesh(mesh.abstract_mesh):
            return mapped(*args)

    return run
```
